128 devices in a mesh: seq: 16 (over z, x), head: 8 (over y, core).
Axes of the slice: x: 4, y: 4, z: 4, core: 2. Of those that a mesh axis runs over, the one named last changes fastest.
Arguments:
- inputs: bfloat16 [16384, 8192], P('seq', 'head'), as said below
- gate_input: bfloat16 [16384, 8192], P('seq', 'head'), may hold values from -6 to 6
- log_decay: float32 [16384, 128], P('seq', 'head'), as said below
- b_matrix: bfloat16 [16384, 8, 128], P('seq', 'head'), may hold values from -6 to 6
- c_matrix: bfloat16 [16384, 8, 128], P('seq', 'head'), may hold values from -1.25 to 1.25
- norm_gain: float32 [8192], P('head'), may hold values from 0.1 to 1.9
- cotangent: bfloat16 [16384, 8192], P('seq', 'head'), may hold values from -6 to 6
Outputs:
- normed: bfloat16 [16384, 8192], P('seq', 'head')
- grad_inputs: bfloat16 [16384, 8192], P('seq', 'head')
- grad_gate: bfloat16 [16384, 8192], P('seq', 'head')
- grad_decay: float32 [16384, 128], P('seq', 'head')
- grad_b_matrix: float32 [16384, 8, 128], P('seq', 'head')
- grad_c_matrix: float32 [16384, 8, 128], P('seq', 'head')
The draws below stay inside these ranges and needn't reach their ends.
Inputs may be any that keep to these rules, and one draw needn't show every extreme that they name: `log_decay`: every entry is strictly negative. `inputs`: real-valued and finite.
All inputs are finite; a program needn't handle non-finite values.
Results may differ from the reference program's by a relative error of at most 0.003.
Values sent between devices are 32-bit elements; how exact they have to be, the bound alone decides.
No kernel may reach another device: no remote copies, remote signals or barrier semaphores. Data moves between devices by JAX's collectives and lax.ppermute only.
A program may use at most 192 MiB of HBM per device.

```python
import math
import jax
import jax.numpy as jnp
from jax import lax

TOK_DEV = 1024
SPAN = 128
P_SIZE = 64
N = 128
TOKEN_TOTAL = 16384
HEAD_TOTAL = 128
GROUPS = 8
WIDTH = 8192


def draw_inputs(key, part):
    key_values, key_cols = jax.random.split(key, 2)
    head_ids = (jnp.arange(WIDTH) // P_SIZE).astype(jnp.float32)
    ramp = head_ids / max(HEAD_TOTAL - 1, 1)
    column_scale = jnp.exp(jax.random.uniform(key_cols, (WIDTH,), minval=0.0, maxval=math.log(4.0)))
    values = jnp.clip(jax.random.normal(key_values, (TOKEN_TOTAL, WIDTH)), -5.0, 5.0)
    values = values * jnp.exp(ramp * math.log(3.0))[None, :]
    return (values * column_scale[None, :]).astype(jnp.bfloat16)


def draw_log_decay(key, part):
    random_subkeys = jax.random.split(key, 7)
    share_slow = 0.5
    slow_heads = jax.random.uniform(random_subkeys[0], (HEAD_TOTAL,)) < share_slow
    fast_rate = jnp.exp(jax.random.uniform(random_subkeys[1], (HEAD_TOTAL,), minval=math.log(1.0 / 50.0), maxval=math.log(1.0 / 30.0)))
    slow_rate = jnp.exp(jax.random.uniform(random_subkeys[2], (HEAD_TOTAL,), minval=math.log(0.1), maxval=math.log(0.5))) / TOKEN_TOTAL
    base_rate = jnp.where(slow_heads, slow_rate, fast_rate)
    shard_factor = jnp.exp(jax.random.uniform(random_subkeys[3], (TOKEN_TOTAL // TOK_DEV, HEAD_TOTAL), minval=math.log(0.5), maxval=math.log(2.0)))
    shard_factor = jnp.repeat(shard_factor, TOK_DEV, axis=0)
    token_factor = jax.random.uniform(random_subkeys[4], (TOKEN_TOTAL, HEAD_TOTAL), minval=0.5, maxval=1.5)
    decay_speed = -base_rate[None, :] * shard_factor * token_factor
    spike_row_list = jax.random.randint(random_subkeys[5], (3,), 0, TOKEN_TOTAL)
    spike_objective = jnp.log(jax.random.uniform(random_subkeys[6], (3, HEAD_TOTAL), minval=0.55, maxval=0.8))
    row_numbers = jnp.arange(TOKEN_TOTAL)[:, None]
    for spike_index in range(3):
        decay_speed = decay_speed + jnp.where(row_numbers == spike_row_list[spike_index], spike_objective[spike_index][None, :], 0.0)
    return decay_speed.astype(jnp.float32)


def block_scale(rng, extent, cuts, smallest, top_value):
    gain, own = 1.0, jax.random.fold_in(rng, 6)
    for position, parts in cuts:
        draws = jnp.exp(jax.random.uniform(jax.random.fold_in(own, position), (parts,), jnp.float32, smallest / len(cuts), top_value / len(cuts)))
        gain = gain * jnp.repeat(draws, extent[position] // parts).reshape([-1 if axis == position else 1 for axis in range(len(extent))])
    return gain


def bell_draw(key, extent, scale, limit, cuts=(), held_as=jnp.bfloat16):
    entries = scale * jax.random.normal(key, extent, jnp.float32)
    if cuts:
        entries = entries * block_scale(key, extent, cuts, -0.22, 0.18)
    return jnp.clip(entries, -limit, limit).astype(held_as)


def setup_inputs(seed: int = 0) -> dict:
    key_list = jax.random.split(jax.random.key(seed), 8)
    return {
        "inputs": draw_inputs(jax.random.fold_in(key_list[7], 71), 0),
        "gate_input": bell_draw(key_list[1], (TOKEN_TOTAL, WIDTH), 1.0, 6.0, ((0, 16), (1, 8))),
        "log_decay": draw_log_decay(jax.random.fold_in(key_list[7], 71), 0),
        "b_matrix": bell_draw(key_list[3], (TOKEN_TOTAL, GROUPS, N), 1.0, 6.0, ((0, 16), (1, 8))),
        "c_matrix": bell_draw(key_list[4], (TOKEN_TOTAL, GROUPS, N), 0.09, 1.25, ((0, 16), (1, 8))),
        "norm_gain": jnp.clip(1.0 + 0.18 * jax.random.normal(key_list[5], (WIDTH,), jnp.float32), 0.1, 1.9),
        "cotangent": bell_draw(key_list[6], (TOKEN_TOTAL, WIDTH), 1.0, 6.0, ((0, 16), (1, 8))),
    }


HIGHEST = lax.Precision.HIGHEST
EPSILON = 1e-05

def pair_scores(c_half, b_half):
    return jnp.einsum('kign,kjgn->kgij', c_half, b_half, preferred_element_type=jnp.float32)

def score_grads(grad_scores, b_blocks, c_blocks):
    grad_c = jnp.einsum('kgij,kjgn->kign', grad_scores, b_blocks, precision=HIGHEST)
    grad_b = jnp.einsum('kgij,kign->kjgn', grad_scores, c_blocks, precision=HIGHEST)
    return (grad_b, grad_c)

def span_core(x_blocks, a_blocks, b_blocks, c_blocks, scores):
    running = jnp.cumsum(jnp.moveaxis(a_blocks, 1, 3), axis=3)
    length = running.shape[3]
    row_numbers = lax.broadcasted_iota(jnp.int32, (length, length), 0)
    col_ids = lax.broadcasted_iota(jnp.int32, (length, length), 1)
    causal = row_numbers >= col_ids
    log_gaps = running[..., :, None] - running[..., None, :]
    decays = jnp.exp(jnp.where(causal, log_gaps, -1e+30))
    weighted = decays * scores[:, :, None]
    diagonal = jnp.einsum('kgrij,kjgrp->kigrp', weighted, x_blocks, precision=HIGHEST)
    span_end = running[..., -1]
    to_end = jnp.exp(span_end[..., None] - running)
    scaled = x_blocks * jnp.moveaxis(to_end, 3, 1)[..., None]
    block_states = jnp.einsum('kjgrp,kjgn->kgrpn', scaled, b_blocks, precision=HIGHEST)

    def advance(carried, paired):
        factor, fresh = paired
        return (factor[..., None, None] * carried + fresh, carried)
    empty_state = jnp.zeros(block_states.shape[1:], jnp.float32)
    final, starts = lax.scan(advance, empty_state, (jnp.exp(span_end), block_states))
    from_state = jnp.einsum('kign,kgrpn->kigrp', c_blocks, starts, precision=HIGHEST)
    ssd_out = diagonal + from_state * jnp.moveaxis(jnp.exp(running), 3, 1)[..., None]
    return (ssd_out, final, running, span_end)

def group_forward(x_blocks, a_blocks, b_blocks, c_blocks, scores):
    return span_core(x_blocks, a_blocks, b_blocks, c_blocks, scores)[0]

def group_apply(packed):
    x_blocks, a_blocks, b_blocks, c_blocks, b_half, c_half = packed
    return group_forward(x_blocks, a_blocks, b_blocks, c_blocks, pair_scores(c_half, b_half))

def group_backward(packed):
    x_blocks, a_blocks, b_blocks, c_blocks, b_half, c_half, upstream = packed
    scores = pair_scores(c_half, b_half)
    unused, pullback = jax.vjp(group_forward, x_blocks, a_blocks, b_blocks, c_blocks, scores)
    grad_x, grad_a, grad_b, grad_c, grad_scores = pullback(upstream)
    extra_b, extra_c = score_grads(grad_scores, b_blocks, c_blocks)
    return (grad_x, grad_a, grad_b + extra_b, grad_c + extra_c)

def reference(inputs, gate_input, log_decay, b_matrix, c_matrix, norm_gain, cotangent):
    tok_rows, width = inputs.shape
    head_count = log_decay.shape[1]
    groups = b_matrix.shape[1]
    state_size = b_matrix.shape[2]
    head_size = width // head_count
    per_group = head_count // groups
    blocks = tok_rows // SPAN
    x_groups = jnp.moveaxis(inputs.astype(jnp.float32).reshape(blocks, SPAN, groups, 1, per_group, head_size), 2, 0)
    a_groups = jnp.moveaxis(log_decay.reshape(blocks, SPAN, groups, 1, per_group), 2, 0)
    b_halves = jnp.moveaxis(b_matrix.reshape(blocks, SPAN, groups, 1, state_size), 2, 0)
    c_halves = jnp.moveaxis(c_matrix.reshape(blocks, SPAN, groups, 1, state_size), 2, 0)
    b_groups = b_halves.astype(jnp.float32)
    c_groups = c_halves.astype(jnp.float32)
    ssd_groups = lax.map(group_apply, (x_groups, a_groups, b_groups, c_groups, b_halves, c_halves))
    ssd_out = jnp.moveaxis(ssd_groups, 0, 2).reshape(tok_rows, width)
    gate_value = gate_input.astype(jnp.float32)
    sigmoid_gate = jax.nn.sigmoid(gate_value)
    gate_silu = gate_value * sigmoid_gate
    gated = ssd_out * gate_silu
    scaled_cot = norm_gain[None, :] * cotangent.astype(jnp.float32)
    squares = lax.optimization_barrier(jnp.sum(gated * gated, axis=1))
    products = lax.optimization_barrier(jnp.sum(gated * scaled_cot, axis=1))
    inverse_rms = lax.rsqrt(squares / width + EPSILON)
    normed = (gated * inverse_rms[:, None] * norm_gain[None, :]).astype(jnp.bfloat16)
    grad_gated = inverse_rms[:, None] * scaled_cot - gated * (inverse_rms ** 3 * products / width)[:, None]
    grad_gate = (grad_gated * ssd_out * sigmoid_gate * (1.0 + gate_value * (1.0 - sigmoid_gate))).astype(jnp.bfloat16)
    grad_ssd = grad_gated * gate_silu
    up_groups = jnp.moveaxis(grad_ssd.reshape(blocks, SPAN, groups, 1, per_group, head_size), 2, 0)
    grad_x, grad_a, grad_b, grad_c = lax.map(group_backward, (x_groups, a_groups, b_groups, c_groups, b_halves, c_halves, up_groups))
    grad_inputs = jnp.moveaxis(grad_x, 0, 2).reshape(tok_rows, width).astype(jnp.bfloat16)
    grad_decay = jnp.moveaxis(grad_a, 0, 2).reshape(tok_rows, head_count)
    grad_b_matrix = jnp.moveaxis(grad_b, 0, 2).reshape(tok_rows, groups, state_size)
    grad_c_matrix = jnp.moveaxis(grad_c, 0, 2).reshape(tok_rows, groups, state_size)
    return (normed, grad_inputs, grad_gate, grad_decay, grad_b_matrix, grad_c_matrix)
```

```python
import jax
import jax.numpy as jnp
from jax import lax
from jax.sharding import PartitionSpec as P

SPAN = 128


HIGHEST = lax.Precision.HIGHEST
EPSILON = 1e-05


def shard_weights(log_carry, reverse):
    count = lax.axis_size("seq")
    place = lax.axis_index("seq")
    ids = jnp.arange(count)
    if reverse:
        source_ok = ids > place
        between = (ids[None, :] > place) & (ids[None, :] < ids[:, None])
    else:
        source_ok = ids < place
        between = (ids[None, :] > ids[:, None]) & (ids[None, :] < place)
    log_gap = jnp.sum(jnp.where(between[:, :, None, None], log_carry[None], 0.0), axis=1)
    return jnp.where(source_ok[:, None, None], jnp.exp(log_gap), 0.0)


def weighted_sum(weights, states):
    return jnp.sum(weights[..., None, None] * states, axis=0)


def pair_scores(c_half, b_half):
    return jnp.einsum("kign,kjgn->kgij", c_half, b_half, preferred_element_type=jnp.float32)


def score_grads(grad_scores, b_blocks, c_blocks):
    grad_c = jnp.einsum("kgij,kjgn->kign", grad_scores, b_blocks, precision=HIGHEST)
    grad_b = jnp.einsum("kgij,kign->kjgn", grad_scores, c_blocks, precision=HIGHEST)
    return (grad_b, grad_c)


def span_core(x_blocks, a_blocks, b_blocks, c_blocks, scores):
    running = jnp.cumsum(jnp.moveaxis(a_blocks, 1, 3), axis=3)
    length = running.shape[3]
    row_numbers = lax.broadcasted_iota(jnp.int32, (length, length), 0)
    col_ids = lax.broadcasted_iota(jnp.int32, (length, length), 1)
    causal = row_numbers >= col_ids
    log_gaps = running[..., :, None] - running[..., None, :]
    decays = jnp.exp(jnp.where(causal, log_gaps, -1e30))
    weighted = decays * scores[:, :, None]
    diagonal = jnp.einsum("kgrij,kjgrp->kigrp", weighted, x_blocks, precision=HIGHEST)
    span_end = running[..., -1]
    to_end = jnp.exp(span_end[..., None] - running)
    scaled = x_blocks * jnp.moveaxis(to_end, 3, 1)[..., None]
    block_states = jnp.einsum("kjgrp,kjgn->kgrpn", scaled, b_blocks, precision=HIGHEST)

    factors = jnp.exp(span_end)
    carried = jnp.zeros(block_states.shape[1:], jnp.float32)
    start_list = []
    for block in range(block_states.shape[0]):
        start_list.append(carried)
        carried = factors[block][..., None, None] * carried + block_states[block]
    final = carried
    starts = jnp.stack(start_list)
    from_state = jnp.einsum("kign,kgrpn->kigrp", c_blocks, starts, precision=HIGHEST)
    ssd_out = diagonal + from_state * jnp.moveaxis(jnp.exp(running), 3, 1)[..., None]
    return (ssd_out, final, running, span_end)


def local_core(x_blocks, a_blocks, b_blocks, c_blocks, scores):
    ssd_part, final, running, span_end = span_core(x_blocks, a_blocks, b_blocks, c_blocks, scores)
    earlier = jnp.cumsum(span_end, axis=0) - span_end
    reach = jnp.exp(running + earlier[..., None])
    log_carry = jnp.sum(span_end, axis=0)
    return (ssd_part, final, reach, jnp.exp(log_carry), log_carry)


def add_incoming(ssd_part, final, reach, carry_all, c_blocks, incoming):
    from_left = jnp.einsum("kgri,kign,grpn->kigrp", reach, c_blocks, incoming, precision=HIGHEST)
    return (ssd_part + from_left, carry_all[..., None, None] * incoming + final)


def per_device(inputs, gate_input, log_decay, b_matrix, c_matrix, norm_gain, cotangent):
    tok_rows, width = inputs.shape
    head_count = log_decay.shape[1]
    groups = b_matrix.shape[1]
    state_size = b_matrix.shape[2]
    head_size = width // head_count
    per_group = head_count // groups
    blocks = tok_rows // SPAN
    full_width = width * lax.axis_size("head")
    x_blocks = inputs.astype(jnp.float32).reshape(blocks, SPAN, groups, per_group, head_size)
    a_blocks = log_decay.reshape(blocks, SPAN, groups, per_group)
    b_half = b_matrix.reshape(blocks, SPAN, groups, state_size)
    c_half = c_matrix.reshape(blocks, SPAN, groups, state_size)
    b_blocks = b_half.astype(jnp.float32)
    c_blocks = c_half.astype(jnp.float32)
    scores = pair_scores(c_half, b_half)
    core_out, core_pull = jax.vjp(local_core, x_blocks, a_blocks, b_blocks, c_blocks, scores)
    ssd_part, final, reach, carry_all, log_carry = core_out
    log_rows = jnp.broadcast_to(log_carry[..., None, None], final.shape[:2] + (8, final.shape[3]))
    packed = lax.all_gather(jnp.concatenate([final, log_rows], axis=2), "seq")
    head_size_p = final.shape[2]
    gathered_final = packed[:, :, :, :head_size_p]
    gathered_log = packed[:, :, :, head_size_p, 0]
    incoming = weighted_sum(shard_weights(gathered_log, False), gathered_final)

    def light_step(part_a, part_b, part_c, part_d, part_e):
        return add_incoming(part_a, part_b, part_c, part_d, part_e, incoming)

    light_out, light_pull = jax.vjp(light_step, ssd_part, final, reach, carry_all, c_blocks)
    ssd_out = light_out[0].reshape(tok_rows, width)
    gate_value = gate_input.astype(jnp.float32)
    sigmoid_gate = jax.nn.sigmoid(gate_value)
    gate_silu = gate_value * sigmoid_gate
    gated = ssd_out * gate_silu
    scaled_cot = norm_gain[None, :] * cotangent.astype(jnp.float32)
    squares, products = lax.psum(
        (jnp.sum(gated * gated, axis=1), jnp.sum(gated * scaled_cot, axis=1)), "head"
    )
    inverse_rms = lax.rsqrt(squares / full_width + EPSILON)
    normed = (gated * inverse_rms[:, None] * norm_gain[None, :]).astype(jnp.bfloat16)
    grad_gated = (
        inverse_rms[:, None] * scaled_cot
        - gated * (inverse_rms**3 * products / full_width)[:, None]
    )
    grad_gate = (
        grad_gated * ssd_out * sigmoid_gate * (1.0 + gate_value * (1.0 - sigmoid_gate))
    ).astype(jnp.bfloat16)
    grad_ssd = grad_gated * gate_silu
    upstream = grad_ssd.reshape(blocks, SPAN, groups, per_group, head_size)
    leaving = jnp.einsum("kgri,kign,kigrp->grpn", reach, c_blocks, upstream, precision=HIGHEST)
    gathered_leaving = lax.all_gather(leaving, "seq")
    adjoint = weighted_sum(shard_weights(gathered_log, True), gathered_leaving)
    light_grads = light_pull((upstream, adjoint))
    grad_x, grad_a, grad_b_core, grad_c_core, grad_scores = core_pull(
        tuple(light_grads[:4]) + (jnp.zeros_like(log_carry),)
    )
    extra_b, extra_c = score_grads(grad_scores, b_blocks, c_blocks)
    grad_b = grad_b_core + extra_b
    grad_c = grad_c_core + extra_c + light_grads[4]
    grad_inputs = grad_x.reshape(tok_rows, width).astype(jnp.bfloat16)
    grad_decay = grad_a.reshape(tok_rows, head_count)
    grad_b_matrix = grad_b.reshape(tok_rows, groups, state_size)
    grad_c_matrix = grad_c.reshape(tok_rows, groups, state_size)
    return (normed, grad_inputs, grad_gate, grad_decay, grad_b_matrix, grad_c_matrix)


def solution(mesh):
    placed = (
        P("seq", "head"),
        P("seq", "head"),
        P("seq", "head"),
        P("seq", "head", None),
        P("seq", "head", None),
        P("head"),
        P("seq", "head"),
    )
    return jax.shard_map(
        per_device,
        mesh=mesh,
        in_specs=placed,
        out_specs=(
            P("seq", "head"),
            P("seq", "head"),
            P("seq", "head"),
            P("seq", "head"),
            P("seq", "head", None),
            P("seq", "head", None),
        ),
        check_vma=False,
    )
```

```python
import jax
import jax.numpy as jnp
from jax import lax
from jax.sharding import PartitionSpec as P


SPAN = 128


HIGHEST = lax.Precision.HIGHEST
EPSILON = 1e-05


def shard_weights(log_carry, reverse):
    count = lax.axis_size("seq")
    place = lax.axis_index("seq")
    ids = jnp.arange(count)
    if reverse:
        source_ok = ids > place
        between = (ids[None, :] > place) & (ids[None, :] < ids[:, None])
    else:
        source_ok = ids < place
        between = (ids[None, :] > ids[:, None]) & (ids[None, :] < place)
    log_gap = jnp.sum(jnp.where(between[:, :, None, None], log_carry[None], 0.0), axis=1)
    return jnp.where(source_ok[:, None, None], jnp.exp(log_gap), 0.0)


def weighted_sum(weights, states):
    total = weights[0][..., None, None] * states[0]
    for source in range(1, states.shape[0]):
        total = total + weights[source][..., None, None] * states[source]
    return total


def pair_scores(c_half, b_half):
    return jnp.einsum("kign,kjgn->kgij", c_half, b_half, preferred_element_type=jnp.float32)


def score_grads(grad_scores, b_blocks, c_blocks):
    grad_c = jnp.einsum("kgij,kjgn->kign", grad_scores, b_blocks, precision=HIGHEST)
    grad_b = jnp.einsum("kgij,kign->kjgn", grad_scores, c_blocks, precision=HIGHEST)
    return (grad_b, grad_c)


def span_core(x_blocks, a_blocks, b_blocks, c_blocks, scores):
    running = jnp.cumsum(jnp.moveaxis(a_blocks, 1, 3), axis=3)
    length = running.shape[3]
    row_numbers = lax.broadcasted_iota(jnp.int32, (length, length), 0)
    col_ids = lax.broadcasted_iota(jnp.int32, (length, length), 1)
    causal = row_numbers >= col_ids
    log_gaps = running[..., :, None] - running[..., None, :]
    decays = jnp.exp(jnp.where(causal, log_gaps, -1e30))
    weighted = decays * scores[:, :, None]
    diagonal = jnp.einsum("kgrij,kjgrp->kigrp", weighted, x_blocks, precision=HIGHEST)
    span_end = running[..., -1]
    to_end = jnp.exp(span_end[..., None] - running)
    scaled = x_blocks * jnp.moveaxis(to_end, 3, 1)[..., None]
    block_states = jnp.einsum("kjgrp,kjgn->kgrpn", scaled, b_blocks, precision=HIGHEST)

    factors = jnp.exp(span_end)
    carried = jnp.zeros(block_states.shape[1:], jnp.float32)
    start_list = []
    for block in range(block_states.shape[0]):
        start_list.append(carried)
        carried = factors[block][..., None, None] * carried + block_states[block]
    final = carried
    starts = jnp.stack(start_list)
    from_state = jnp.einsum("kign,kgrpn->kigrp", c_blocks, starts, precision=HIGHEST)
    ssd_out = diagonal + from_state * jnp.moveaxis(jnp.exp(running), 3, 1)[..., None]
    return (ssd_out, final, running, span_end)


def local_core(x_blocks, a_blocks, b_blocks, c_blocks, scores):
    ssd_part, final, running, span_end = span_core(x_blocks, a_blocks, b_blocks, c_blocks, scores)
    earlier = jnp.cumsum(span_end, axis=0) - span_end
    reach = jnp.exp(running + earlier[..., None])
    log_carry = jnp.sum(span_end, axis=0)
    return (ssd_part, final, reach, jnp.exp(log_carry), log_carry)


def add_incoming(ssd_part, final, reach, carry_all, c_blocks, incoming):
    projected = jnp.einsum("kign,grpn->kigrp", c_blocks, incoming, precision=HIGHEST)
    from_left = projected * jnp.moveaxis(reach, 3, 1)[..., None]
    return (ssd_part + from_left, carry_all[..., None, None] * incoming + final)


def device_body(inputs, gate_input, log_decay, b_matrix, c_matrix, norm_gain, cotangent):
    tok_rows, width = inputs.shape
    head_count = log_decay.shape[1]
    groups = b_matrix.shape[1]
    state_size = b_matrix.shape[2]
    head_size = width // head_count
    per_group = head_count // groups
    blocks = tok_rows // SPAN
    full_width = width * lax.axis_size("head")
    x_blocks = inputs.astype(jnp.float32).reshape(blocks, SPAN, groups, per_group, head_size)
    a_blocks = log_decay.reshape(blocks, SPAN, groups, per_group)
    b_half = b_matrix.reshape(blocks, SPAN, groups, state_size)
    c_half = c_matrix.reshape(blocks, SPAN, groups, state_size)
    b_blocks = b_half.astype(jnp.float32)
    c_blocks = c_half.astype(jnp.float32)
    scores = pair_scores(c_half, b_half)
    core_out, core_pull = jax.vjp(local_core, x_blocks, a_blocks, b_blocks, c_blocks, scores)
    ssd_part, final, reach, carry_all, log_carry = core_out
    ssd_part = lax.optimization_barrier(ssd_part)
    log_rows = jnp.broadcast_to(log_carry[..., None, None], final.shape[:2] + (8, final.shape[3]))
    packed = lax.all_gather(jnp.concatenate([final, log_rows], axis=2), "seq")
    head_size_p = final.shape[2]
    gathered_log = jnp.max(packed[:, :, :, head_size_p:], axis=(3, 4))
    incoming = weighted_sum(shard_weights(gathered_log, False), packed)[:, :, :head_size_p]

    def light_step(part_a, part_b, part_c, part_d, part_e):
        return add_incoming(part_a, part_b, part_c, part_d, part_e, incoming)

    light_out, light_pull = jax.vjp(light_step, ssd_part, final, reach, carry_all, c_blocks)
    ssd_out = light_out[0].reshape(tok_rows, width)
    gate_value = gate_input.astype(jnp.float32)
    sigmoid_gate = jax.nn.sigmoid(gate_value)
    gate_silu = gate_value * sigmoid_gate
    gated = ssd_out * gate_silu
    scaled_cot = norm_gain[None, :] * cotangent.astype(jnp.float32)
    squares, products = lax.psum(
        (jnp.sum(gated * gated, axis=1), jnp.sum(gated * scaled_cot, axis=1)), "head"
    )
    inverse_rms = lax.rsqrt(squares / full_width + EPSILON)
    normed = (gated * inverse_rms[:, None] * norm_gain[None, :]).astype(jnp.bfloat16)
    grad_gated = (
        inverse_rms[:, None] * scaled_cot
        - gated * (inverse_rms**3 * products / full_width)[:, None]
    )
    grad_gate = (
        grad_gated * ssd_out * sigmoid_gate * (1.0 + gate_value * (1.0 - sigmoid_gate))
    ).astype(jnp.bfloat16)
    grad_ssd = grad_gated * gate_silu
    upstream = grad_ssd.reshape(blocks, SPAN, groups, per_group, head_size)
    reached = upstream * jnp.moveaxis(reach, 3, 1)[..., None]
    leaving = jnp.einsum("kign,kigrp->grpn", c_blocks, reached, precision=HIGHEST)
    gathered_leaving = lax.all_gather(leaving, "seq")
    adjoint = weighted_sum(shard_weights(gathered_log, True), gathered_leaving)
    light_grads = light_pull((upstream, adjoint))
    grad_x, grad_a, grad_b_core, grad_c_core, grad_scores = core_pull(
        tuple(light_grads[:4]) + (jnp.zeros_like(log_carry),)
    )
    extra_b, extra_c = score_grads(grad_scores, b_blocks, c_blocks)
    grad_b = grad_b_core + extra_b
    grad_c = grad_c_core + extra_c + light_grads[4]
    grad_inputs = grad_x.reshape(tok_rows, width).astype(jnp.bfloat16)
    grad_decay = grad_a.reshape(tok_rows, head_count)
    grad_b_matrix = grad_b.reshape(tok_rows, groups, state_size)
    grad_c_matrix = grad_c.reshape(tok_rows, groups, state_size)
    return (normed, grad_inputs, grad_gate, grad_decay, grad_b_matrix, grad_c_matrix)


def solution(mesh):
    placed = (
        P("seq", "head"),
        P("seq", "head"),
        P("seq", "head"),
        P("seq", "head", None),
        P("seq", "head", None),
        P("head"),
        P("seq", "head"),
    )
    return jax.shard_map(
        device_body,
        mesh=mesh,
        in_specs=placed,
        out_specs=(
            P("seq", "head"),
            P("seq", "head"),
            P("seq", "head"),
            P("seq", "head"),
            P("seq", "head", None),
            P("seq", "head", None),
        ),
        check_vma=False,
    )
```

```python
import jax
import jax.numpy as jnp
from jax import lax
from jax.sharding import PartitionSpec as P


SPAN = 128


PRECISION = lax.Precision.HIGH
EPSILON = 1e-05


def shard_weights(log_carry, reverse):
    count = lax.axis_size("seq")
    place = lax.axis_index("seq")
    ids = jnp.arange(count)
    if reverse:
        source_ok = ids > place
        between = (ids[None, :] > place) & (ids[None, :] < ids[:, None])
    else:
        source_ok = ids < place
        between = (ids[None, :] > ids[:, None]) & (ids[None, :] < place)
    log_gap = jnp.sum(jnp.where(between[:, :, None, None], log_carry[None], 0.0), axis=1)
    return jnp.where(source_ok[:, None, None], jnp.exp(log_gap), 0.0)


def weighted_sum(weights, states):
    total = weights[0][..., None, None] * states[0]
    for source in range(1, states.shape[0]):
        total = total + weights[source][..., None, None] * states[source]
    return total


def pair_scores(c_half, b_half):
    return jnp.einsum("kign,kjgn->kgij", c_half, b_half, preferred_element_type=jnp.float32)


def score_grads(grad_scores, b_blocks, c_blocks):
    grad_c = jnp.einsum("kgij,kjgn->kign", grad_scores, b_blocks, precision=PRECISION)
    grad_b = jnp.einsum("kgij,kign->kjgn", grad_scores, c_blocks, precision=PRECISION)
    return (grad_b, grad_c)


def span_core(x_blocks, a_blocks, b_blocks, c_blocks, scores):
    running = jnp.cumsum(jnp.moveaxis(a_blocks, 1, 3), axis=3)
    length = running.shape[3]
    row_numbers = lax.broadcasted_iota(jnp.int32, (length, length), 0)
    col_ids = lax.broadcasted_iota(jnp.int32, (length, length), 1)
    causal = row_numbers >= col_ids
    log_gaps = running[..., :, None] - running[..., None, :]
    decays = jnp.exp(jnp.where(causal, log_gaps, -1e30))
    weighted = decays * scores[:, :, None]
    diagonal = jnp.einsum("kgrij,kjgrp->kigrp", weighted, x_blocks, precision=PRECISION)
    span_end = running[..., -1]
    to_end = jnp.exp(span_end[..., None] - running)
    scaled = x_blocks * jnp.moveaxis(to_end, 3, 1)[..., None]
    block_states = jnp.einsum("kjgrp,kjgn->kgrpn", scaled, b_blocks, precision=PRECISION)

    factors = jnp.exp(span_end)
    carried = jnp.zeros(block_states.shape[1:], jnp.float32)
    start_list = []
    for block in range(block_states.shape[0]):
        start_list.append(carried)
        carried = factors[block][..., None, None] * carried + block_states[block]
    final = carried
    starts = jnp.stack(start_list)
    from_state = jnp.einsum("kign,kgrpn->kigrp", c_blocks, starts, precision=PRECISION)
    ssd_out = diagonal + from_state * jnp.moveaxis(jnp.exp(running), 3, 1)[..., None]
    return (ssd_out, final, running, span_end)


def local_core(x_blocks, a_blocks, b_blocks, c_blocks, scores):
    ssd_part, final, running, span_end = span_core(x_blocks, a_blocks, b_blocks, c_blocks, scores)
    earlier = jnp.cumsum(span_end, axis=0) - span_end
    reach = jnp.exp(running + earlier[..., None])
    log_carry = jnp.sum(span_end, axis=0)
    return (ssd_part, final, reach, jnp.exp(log_carry), log_carry)


def add_incoming(ssd_part, final, reach, carry_all, c_blocks, incoming):
    projected = jnp.einsum("kign,grpn->kigrp", c_blocks, incoming, precision=PRECISION)
    from_left = projected * jnp.moveaxis(reach, 3, 1)[..., None]
    return (ssd_part + from_left, carry_all[..., None, None] * incoming + final)


def device_body(inputs, gate_input, log_decay, b_matrix, c_matrix, norm_gain, cotangent):
    tok_rows, width = inputs.shape
    head_count = log_decay.shape[1]
    groups = b_matrix.shape[1]
    state_size = b_matrix.shape[2]
    head_size = width // head_count
    per_group = head_count // groups
    blocks = tok_rows // SPAN
    full_width = width * lax.axis_size("head")
    x_blocks = inputs.astype(jnp.float32).reshape(blocks, SPAN, groups, per_group, head_size)
    a_blocks = log_decay.reshape(blocks, SPAN, groups, per_group)
    b_half = b_matrix.reshape(blocks, SPAN, groups, state_size)
    c_half = c_matrix.reshape(blocks, SPAN, groups, state_size)
    b_blocks = b_half.astype(jnp.float32)
    c_blocks = c_half.astype(jnp.float32)
    scores = pair_scores(c_half, b_half)
    core_out, core_pull = jax.vjp(local_core, x_blocks, a_blocks, b_blocks, c_blocks, scores)
    ssd_part, final, reach, carry_all, log_carry = core_out
    ssd_part = lax.optimization_barrier(ssd_part)
    log_rows = jnp.broadcast_to(log_carry[..., None, None], final.shape[:2] + (8, final.shape[3]))
    packed = lax.all_gather(jnp.concatenate([final, log_rows], axis=2), "seq")
    head_size_p = final.shape[2]
    gathered_log = jnp.max(packed[:, :, :, head_size_p:], axis=(3, 4))
    incoming = weighted_sum(shard_weights(gathered_log, False), packed)[:, :, :head_size_p]

    def light_step(part_a, part_b, part_c, part_d, part_e):
        return add_incoming(part_a, part_b, part_c, part_d, part_e, incoming)

    light_out, light_pull = jax.vjp(light_step, ssd_part, final, reach, carry_all, c_blocks)
    ssd_out = light_out[0].reshape(tok_rows, width)
    gate_value = gate_input.astype(jnp.float32)
    sigmoid_gate = jax.nn.sigmoid(gate_value)
    gate_silu = gate_value * sigmoid_gate
    gated = ssd_out * gate_silu
    scaled_cot = norm_gain[None, :] * cotangent.astype(jnp.float32)
    squares, products = lax.psum(
        (jnp.sum(gated * gated, axis=1), jnp.sum(gated * scaled_cot, axis=1)), "head"
    )
    inverse_rms = lax.rsqrt(squares / full_width + EPSILON)
    normed = (gated * inverse_rms[:, None] * norm_gain[None, :]).astype(jnp.bfloat16)
    grad_gated = (
        inverse_rms[:, None] * scaled_cot
        - gated * (inverse_rms**3 * products / full_width)[:, None]
    )
    grad_gate = (
        grad_gated * ssd_out * sigmoid_gate * (1.0 + gate_value * (1.0 - sigmoid_gate))
    ).astype(jnp.bfloat16)
    grad_ssd = grad_gated * gate_silu
    upstream = grad_ssd.reshape(blocks, SPAN, groups, per_group, head_size)
    reached = upstream * jnp.moveaxis(reach, 3, 1)[..., None]
    leaving = jnp.einsum("kign,kigrp->grpn", c_blocks, reached, precision=PRECISION)
    gathered_leaving = lax.all_gather(leaving, "seq")
    adjoint = weighted_sum(shard_weights(gathered_log, True), gathered_leaving)
    light_grads = light_pull((upstream, adjoint))
    grad_x, grad_a, grad_b_core, grad_c_core, grad_scores = core_pull(
        tuple(light_grads[:4]) + (jnp.zeros_like(log_carry),)
    )
    extra_b, extra_c = score_grads(grad_scores, b_blocks, c_blocks)
    grad_b = grad_b_core + extra_b
    grad_c = grad_c_core + extra_c + light_grads[4]
    grad_inputs = grad_x.reshape(tok_rows, width).astype(jnp.bfloat16)
    grad_decay = grad_a.reshape(tok_rows, head_count)
    grad_b_matrix = grad_b.reshape(tok_rows, groups, state_size)
    grad_c_matrix = grad_c.reshape(tok_rows, groups, state_size)
    return (normed, grad_inputs, grad_gate, grad_decay, grad_b_matrix, grad_c_matrix)


def solution(mesh):
    placed = (
        P("seq", "head"),
        P("seq", "head"),
        P("seq", "head"),
        P("seq", "head", None),
        P("seq", "head", None),
        P("head"),
        P("seq", "head"),
    )
    return jax.shard_map(
        device_body,
        mesh=mesh,
        in_specs=placed,
        out_specs=(
            P("seq", "head"),
            P("seq", "head"),
            P("seq", "head"),
            P("seq", "head"),
            P("seq", "head", None),
            P("seq", "head", None),
        ),
        check_vma=False,
    )
```

```python
import jax
import jax.numpy as jnp
from jax import lax
from jax.sharding import PartitionSpec as P


SPAN = 128


PRECISION = lax.Precision.HIGH
EPSILON = 1e-05


def shard_weights(log_carry, reverse):
    count = lax.axis_size("seq")
    place = lax.axis_index("seq")
    ids = jnp.arange(count)
    if reverse:
        source_ok = ids > place
        between = (ids[None, :] > place) & (ids[None, :] < ids[:, None])
    else:
        source_ok = ids < place
        between = (ids[None, :] > ids[:, None]) & (ids[None, :] < place)
    log_gap = jnp.sum(jnp.where(between[:, :, None, None], log_carry[None], 0.0), axis=1)
    return jnp.where(source_ok[:, None, None], jnp.exp(log_gap), 0.0)


def weighted_sum(weights, states):
    total = weights[0][..., None, None] * states[0]
    for source in range(1, states.shape[0]):
        total = total + weights[source][..., None, None] * states[source]
    return total


def pair_scores(c_half, b_half):
    return jnp.einsum("kign,kjgn->kgij", c_half, b_half, preferred_element_type=jnp.float32)


def score_grads(grad_scores, b_blocks, c_blocks):
    grad_c = jnp.einsum("kgij,kjgn->kign", grad_scores, b_blocks, precision=PRECISION)
    grad_b = jnp.einsum("kgij,kign->kjgn", grad_scores, c_blocks, precision=PRECISION)
    return (grad_b, grad_c)


def block_chain(x_blocks, a_blocks, b_blocks):
    running = jnp.cumsum(jnp.moveaxis(a_blocks, 1, 3), axis=3)
    span_end = running[..., -1]
    to_end = jnp.exp(span_end[..., None] - running)
    scaled = x_blocks * jnp.moveaxis(to_end, 3, 1)[..., None]
    block_states = jnp.einsum("kjgrp,kjgn->kgrpn", scaled, b_blocks, precision=PRECISION)
    factors = jnp.exp(span_end)
    carried = jnp.zeros(block_states.shape[1:], jnp.float32)
    start_list = []
    for block in range(block_states.shape[0]):
        start_list.append(carried)
        carried = factors[block][..., None, None] * carried + block_states[block]
    return (running, span_end, jnp.stack(start_list), carried)


def local_core(x_blocks, a_blocks, b_blocks, c_blocks, scores):
    running, span_end, starts, _ = block_chain(x_blocks, a_blocks, b_blocks)
    length = running.shape[3]
    row_numbers = lax.broadcasted_iota(jnp.int32, (length, length), 0)
    col_ids = lax.broadcasted_iota(jnp.int32, (length, length), 1)
    causal = row_numbers >= col_ids
    log_gaps = running[..., :, None] - running[..., None, :]
    decays = jnp.exp(jnp.where(causal, log_gaps, -1e30))
    weighted = decays * scores[:, :, None]
    diagonal = jnp.einsum("kgrij,kjgrp->kigrp", weighted, x_blocks, precision=PRECISION)
    from_state = jnp.einsum("kign,kgrpn->kigrp", c_blocks, starts, precision=PRECISION)
    ssd_part = diagonal + from_state * jnp.moveaxis(jnp.exp(running), 3, 1)[..., None]
    earlier = jnp.cumsum(span_end, axis=0) - span_end
    reach = jnp.exp(running + earlier[..., None])
    return (ssd_part, reach)


def edge_grads(adjoint, carry_grad, x_blocks, b_blocks, to_end, later, carry_all):
    tokens = x_blocks.shape[0] * x_blocks.shape[1]
    x_tok = x_blocks.reshape((tokens,) + x_blocks.shape[2:])
    b_tok = b_blocks.reshape((tokens,) + b_blocks.shape[2:])
    weights = jnp.exp(jnp.moveaxis(to_end + later[..., None], 3, 1))
    weights = weights.reshape((tokens,) + weights.shape[2:])
    projected = jnp.einsum("tgn,grpn->tgrp", b_tok, adjoint, precision=PRECISION)
    grad_x = weights[..., None] * projected
    log_grad = weights * jnp.sum(x_tok * projected, axis=3)
    grad_b = jnp.einsum("tgrp,grpn->tgn", weights[..., None] * x_tok, adjoint, precision=PRECISION)
    grad_a = jnp.cumsum(log_grad, axis=0) - log_grad + (carry_grad * carry_all)[None]
    return (
        grad_x.reshape(x_blocks.shape),
        grad_a.reshape(x_blocks.shape[:4]),
        grad_b.reshape(b_blocks.shape),
    )


def add_incoming(ssd_part, reach, c_blocks, incoming):
    projected = jnp.einsum("kign,grpn->kigrp", c_blocks, incoming, precision=PRECISION)
    return ssd_part + projected * jnp.moveaxis(reach, 3, 1)[..., None]


def device_body(inputs, gate_input, log_decay, b_matrix, c_matrix, norm_gain, cotangent):
    tok_rows, width = inputs.shape
    head_count = log_decay.shape[1]
    groups = b_matrix.shape[1]
    state_size = b_matrix.shape[2]
    head_size = width // head_count
    per_group = head_count // groups
    blocks = tok_rows // SPAN
    full_width = width * lax.axis_size("head")
    x_blocks = inputs.astype(jnp.float32).reshape(blocks, SPAN, groups, per_group, head_size)
    a_blocks = log_decay.reshape(blocks, SPAN, groups, per_group)
    b_half = b_matrix.reshape(blocks, SPAN, groups, state_size)
    c_half = c_matrix.reshape(blocks, SPAN, groups, state_size)
    b_blocks = b_half.astype(jnp.float32)
    c_blocks = c_half.astype(jnp.float32)
    scores = pair_scores(c_half, b_half)
    core_out, core_pull = jax.vjp(local_core, x_blocks, a_blocks, b_blocks, c_blocks, scores)
    ssd_part, reach = core_out
    ssd_part = lax.optimization_barrier(ssd_part)
    running, span_end, _, final = block_chain(x_blocks, a_blocks, b_blocks)
    carry_all = jnp.exp(jnp.sum(span_end, axis=0))
    to_end = span_end[..., None] - running
    later = jnp.cumsum(span_end[::-1], axis=0)[::-1] - span_end
    log_carry = jnp.sum(a_blocks, axis=(0, 1))
    log_rows = jnp.broadcast_to(log_carry[..., None, None], final.shape[:2] + (8, final.shape[3]))
    packed = lax.all_gather(jnp.concatenate([final, log_rows], axis=2), "seq")
    head_size_p = final.shape[2]
    gathered_log = jnp.max(packed[:, :, :, head_size_p:], axis=(3, 4))
    incoming = weighted_sum(shard_weights(gathered_log, False), packed)[:, :, :head_size_p]

    def light_step(part_a, part_b, part_c):
        return add_incoming(part_a, part_b, part_c, incoming)

    light_out, light_pull = jax.vjp(light_step, ssd_part, reach, c_blocks)
    ssd_out = light_out.reshape(tok_rows, width)
    gate_value = gate_input.astype(jnp.float32)
    sigmoid_gate = jax.nn.sigmoid(gate_value)
    gate_silu = gate_value * sigmoid_gate
    scaled_cot = norm_gain[None, :] * cotangent.astype(jnp.float32)
    gated = ssd_out * gate_silu
    squares, products = lax.psum(
        (jnp.sum(gated * gated, axis=1), jnp.sum(gated * scaled_cot, axis=1)), "head"
    )
    inverse_rms = lax.rsqrt(squares / full_width + EPSILON)
    normed = (gated * inverse_rms[:, None] * norm_gain[None, :]).astype(jnp.bfloat16)
    grad_gated = (
        inverse_rms[:, None] * scaled_cot
        - gated * (inverse_rms**3 * products / full_width)[:, None]
    )
    grad_gate = (
        grad_gated * ssd_out * sigmoid_gate * (1.0 + gate_value * (1.0 - sigmoid_gate))
    ).astype(jnp.bfloat16)
    grad_ssd = grad_gated * gate_silu
    upstream = grad_ssd.reshape(blocks, SPAN, groups, per_group, head_size)
    reached = upstream * jnp.moveaxis(reach, 3, 1)[..., None]
    leaving = jnp.einsum("kign,kigrp->grpn", c_blocks, reached, precision=PRECISION)
    gathered_leaving = lax.all_gather(leaving, "seq")
    adjoint = weighted_sum(shard_weights(gathered_log, True), gathered_leaving)
    light_grads = light_pull(upstream)
    core_grads = lax.optimization_barrier(core_pull(tuple(light_grads[:2])))
    carry_grad = jnp.sum(adjoint * incoming, axis=(2, 3))
    edge_x, edge_a, edge_b = edge_grads(
        adjoint, carry_grad, x_blocks, b_blocks, to_end, later, carry_all
    )
    grad_x_core, grad_a_core, grad_b_core, grad_c_core, grad_scores = core_grads
    extra_b, extra_c = score_grads(grad_scores, b_blocks, c_blocks)
    grad_x = grad_x_core + edge_x
    grad_a = grad_a_core + edge_a
    grad_b = grad_b_core + extra_b + edge_b
    grad_c = grad_c_core + extra_c + light_grads[2]
    grad_inputs = grad_x.reshape(tok_rows, width).astype(jnp.bfloat16)
    grad_decay = grad_a.reshape(tok_rows, head_count)
    grad_b_matrix = grad_b.reshape(tok_rows, groups, state_size)
    grad_c_matrix = grad_c.reshape(tok_rows, groups, state_size)
    return (normed, grad_inputs, grad_gate, grad_decay, grad_b_matrix, grad_c_matrix)


def solution(mesh):
    placed = (
        P("seq", "head"),
        P("seq", "head"),
        P("seq", "head"),
        P("seq", "head", None),
        P("seq", "head", None),
        P("head"),
        P("seq", "head"),
    )
    return jax.shard_map(
        device_body,
        mesh=mesh,
        in_specs=placed,
        out_specs=(
            P("seq", "head"),
            P("seq", "head"),
            P("seq", "head"),
            P("seq", "head"),
            P("seq", "head", None),
            P("seq", "head", None),
        ),
        check_vma=False,
    )
```

```python
import jax
import jax.numpy as jnp
from jax import lax
from jax.sharding import PartitionSpec as P


SPAN = 128


PRECISION = lax.Precision.HIGH
EPSILON = 1e-05


ROW = 4


def gap_weights(log_carry, place, later):
    ids = jnp.arange(log_carry.shape[0])
    if later:
        source_ok = ids > place
        between = (ids[None, :] > place) & (ids[None, :] < ids[:, None])
    else:
        source_ok = ids < place
        between = (ids[None, :] > ids[:, None]) & (ids[None, :] < place)
    log_gap = jnp.sum(jnp.where(between[:, :, None, None], log_carry[None], 0.0), axis=1)
    return jnp.where(source_ok[:, None, None], jnp.exp(log_gap), 0.0)


def tile_logs(log_carry, like):
    return jnp.broadcast_to(log_carry[..., None, None], like.shape[:2] + (8, like.shape[3]))


def grouped_gather(value, groups):
    return lax.all_gather(value, "seq", axis_index_groups=groups)


def seq_groups():
    count = lax.axis_size("seq")
    rows = count // ROW
    row_groups = [[z * ROW + x for x in range(ROW)] for z in range(rows)]
    col_groups = [[z * ROW + x for z in range(rows)] for x in range(ROW)]
    return row_groups, col_groups


def prefix_state(final, log_carry):
    place = lax.axis_index("seq")
    col, row = place % ROW, place // ROW
    row_groups, col_groups = seq_groups()
    size = final.shape[2]
    row_all = grouped_gather(jnp.concatenate([final, tile_logs(log_carry, final)], axis=2), row_groups)
    row_logs = jnp.max(row_all[:, :, :, size:], axis=(3, 4))
    in_row = weighted_sum(gap_weights(row_logs, col, False), row_all)[:, :, :size]
    row_total = weighted_sum(gap_weights(row_logs, ROW, False), row_all)[:, :, :size]
    row_log = jnp.sum(row_logs, axis=0)
    col_all = grouped_gather(jnp.concatenate([row_total, tile_logs(row_log, final)], axis=2), col_groups)
    col_logs = jnp.max(col_all[:, :, :, size:], axis=(3, 4))
    before_row = weighted_sum(gap_weights(col_logs, row, False), col_all)[:, :, :size]
    into_row = jnp.sum(jnp.where((jnp.arange(ROW) < col)[:, None, None], row_logs, 0.0), axis=0)
    incoming = in_row + jnp.exp(into_row)[..., None, None] * before_row
    return incoming, (row_logs, col_logs)


def suffix_state(leaving, logs):
    row_logs, col_logs = logs
    place = lax.axis_index("seq")
    col, row = place % ROW, place // ROW
    row_groups, col_groups = seq_groups()
    row_all = grouped_gather(leaving, row_groups)
    in_row = weighted_sum(gap_weights(row_logs, col, True), row_all)
    row_head = weighted_sum(gap_weights(row_logs, -1, True), row_all)
    col_all = grouped_gather(row_head, col_groups)
    after_row = weighted_sum(gap_weights(col_logs, row, True), col_all)
    out_of_row = jnp.sum(jnp.where((jnp.arange(ROW) > col)[:, None, None], row_logs, 0.0), axis=0)
    return in_row + jnp.exp(out_of_row)[..., None, None] * after_row


def weighted_sum(weights, states):
    total = weights[0][..., None, None] * states[0]
    for source in range(1, states.shape[0]):
        total = total + weights[source][..., None, None] * states[source]
    return total


def pair_scores(c_half, b_half):
    return jnp.einsum("kign,kjgn->kgij", c_half, b_half, preferred_element_type=jnp.float32)


def score_grads(grad_scores, b_blocks, c_blocks):
    grad_c = jnp.einsum("kgij,kjgn->kign", grad_scores, b_blocks, precision=PRECISION)
    grad_b = jnp.einsum("kgij,kign->kjgn", grad_scores, c_blocks, precision=PRECISION)
    return (grad_b, grad_c)


def block_chain(x_blocks, a_blocks, b_blocks):
    running = jnp.cumsum(jnp.moveaxis(a_blocks, 1, 3), axis=3)
    span_end = running[..., -1]
    to_end = jnp.exp(span_end[..., None] - running)
    scaled = x_blocks * jnp.moveaxis(to_end, 3, 1)[..., None]
    block_states = jnp.einsum("kjgrp,kjgn->kgrpn", scaled, b_blocks, precision=PRECISION)
    factors = jnp.exp(span_end)
    carried = jnp.zeros(block_states.shape[1:], jnp.float32)
    start_list = []
    for block in range(block_states.shape[0]):
        start_list.append(carried)
        carried = factors[block][..., None, None] * carried + block_states[block]
    return (running, span_end, jnp.stack(start_list), carried)


def local_core(x_blocks, a_blocks, b_blocks, c_blocks, scores):
    running, span_end, starts, _ = block_chain(x_blocks, a_blocks, b_blocks)
    length = running.shape[3]
    row_numbers = lax.broadcasted_iota(jnp.int32, (length, length), 0)
    col_ids = lax.broadcasted_iota(jnp.int32, (length, length), 1)
    causal = row_numbers >= col_ids
    log_gaps = running[..., :, None] - running[..., None, :]
    decays = jnp.exp(jnp.where(causal, log_gaps, -1e30))
    weighted = decays * scores[:, :, None]
    diagonal = jnp.einsum("kgrij,kjgrp->kigrp", weighted, x_blocks, precision=PRECISION)
    from_state = jnp.einsum("kign,kgrpn->kigrp", c_blocks, starts, precision=PRECISION)
    ssd_part = diagonal + from_state * jnp.moveaxis(jnp.exp(running), 3, 1)[..., None]
    earlier = jnp.cumsum(span_end, axis=0) - span_end
    reach = jnp.exp(running + earlier[..., None])
    return (ssd_part, reach)


def edge_grads(adjoint, carry_grad, x_blocks, b_blocks, to_end, later, carry_all):
    tokens = x_blocks.shape[0] * x_blocks.shape[1]
    x_tok = x_blocks.reshape((tokens,) + x_blocks.shape[2:])
    b_tok = b_blocks.reshape((tokens,) + b_blocks.shape[2:])
    weights = jnp.exp(jnp.moveaxis(to_end + later[..., None], 3, 1))
    weights = weights.reshape((tokens,) + weights.shape[2:])
    projected = jnp.einsum("tgn,grpn->tgrp", b_tok, adjoint, precision=PRECISION)
    grad_x = weights[..., None] * projected
    log_grad = weights * jnp.sum(x_tok * projected, axis=3)
    grad_b = jnp.einsum("tgrp,grpn->tgn", weights[..., None] * x_tok, adjoint, precision=PRECISION)
    grad_a = jnp.cumsum(log_grad, axis=0) - log_grad + (carry_grad * carry_all)[None]
    return (
        grad_x.reshape(x_blocks.shape),
        grad_a.reshape(x_blocks.shape[:4]),
        grad_b.reshape(b_blocks.shape),
    )


def add_incoming(ssd_part, reach, c_blocks, incoming):
    projected = jnp.einsum("kign,grpn->kigrp", c_blocks, incoming, precision=PRECISION)
    return ssd_part + projected * jnp.moveaxis(reach, 3, 1)[..., None]


def device_body(inputs, gate_input, log_decay, b_matrix, c_matrix, norm_gain, cotangent):
    tok_rows, width = inputs.shape
    head_count = log_decay.shape[1]
    groups = b_matrix.shape[1]
    state_size = b_matrix.shape[2]
    head_size = width // head_count
    per_group = head_count // groups
    blocks = tok_rows // SPAN
    full_width = width * lax.axis_size("head")
    x_blocks = inputs.astype(jnp.float32).reshape(blocks, SPAN, groups, per_group, head_size)
    a_blocks = log_decay.reshape(blocks, SPAN, groups, per_group)
    b_half = b_matrix.reshape(blocks, SPAN, groups, state_size)
    c_half = c_matrix.reshape(blocks, SPAN, groups, state_size)
    b_blocks = b_half.astype(jnp.float32)
    c_blocks = c_half.astype(jnp.float32)
    scores = pair_scores(c_half, b_half)
    core_out, core_pull = jax.vjp(local_core, x_blocks, a_blocks, b_blocks, c_blocks, scores)
    ssd_part, reach = core_out
    ssd_part = lax.optimization_barrier(ssd_part)
    running, span_end, _, final = block_chain(x_blocks, a_blocks, b_blocks)
    carry_all = jnp.exp(jnp.sum(span_end, axis=0))
    to_end = span_end[..., None] - running
    later = jnp.cumsum(span_end[::-1], axis=0)[::-1] - span_end
    log_carry = jnp.sum(a_blocks, axis=(0, 1))
    incoming, seq_logs = prefix_state(final, log_carry)

    def light_step(part_a, part_b, part_c):
        return add_incoming(part_a, part_b, part_c, incoming)

    light_out, light_pull = jax.vjp(light_step, ssd_part, reach, c_blocks)
    ssd_out = light_out.reshape(tok_rows, width)
    gate_value = gate_input.astype(jnp.float32)
    sigmoid_gate = jax.nn.sigmoid(gate_value)
    gate_silu = gate_value * sigmoid_gate
    scaled_cot = norm_gain[None, :] * cotangent.astype(jnp.float32)
    gated = ssd_out * gate_silu
    squares, products = lax.psum(
        (jnp.sum(gated * gated, axis=1), jnp.sum(gated * scaled_cot, axis=1)), "head"
    )
    inverse_rms = lax.rsqrt(squares / full_width + EPSILON)
    normed = (gated * inverse_rms[:, None] * norm_gain[None, :]).astype(jnp.bfloat16)
    grad_gated = (
        inverse_rms[:, None] * scaled_cot
        - gated * (inverse_rms**3 * products / full_width)[:, None]
    )
    grad_gate = (
        grad_gated * ssd_out * sigmoid_gate * (1.0 + gate_value * (1.0 - sigmoid_gate))
    ).astype(jnp.bfloat16)
    grad_ssd = grad_gated * gate_silu
    upstream = grad_ssd.reshape(blocks, SPAN, groups, per_group, head_size)
    reached = upstream * jnp.moveaxis(reach, 3, 1)[..., None]
    leaving = jnp.einsum("kign,kigrp->grpn", c_blocks, reached, precision=PRECISION)
    adjoint = suffix_state(leaving, seq_logs)
    light_grads = light_pull(upstream)
    core_grads = lax.optimization_barrier(core_pull(tuple(light_grads[:2])))
    carry_grad = jnp.sum(adjoint * incoming, axis=(2, 3))
    edge_x, edge_a, edge_b = edge_grads(
        adjoint, carry_grad, x_blocks, b_blocks, to_end, later, carry_all
    )
    grad_x_core, grad_a_core, grad_b_core, grad_c_core, grad_scores = core_grads
    extra_b, extra_c = score_grads(grad_scores, b_blocks, c_blocks)
    grad_x = grad_x_core + edge_x
    grad_a = grad_a_core + edge_a
    grad_b = grad_b_core + extra_b + edge_b
    grad_c = grad_c_core + extra_c + light_grads[2]
    grad_inputs = grad_x.reshape(tok_rows, width).astype(jnp.bfloat16)
    grad_decay = grad_a.reshape(tok_rows, head_count)
    grad_b_matrix = grad_b.reshape(tok_rows, groups, state_size)
    grad_c_matrix = grad_c.reshape(tok_rows, groups, state_size)
    return (normed, grad_inputs, grad_gate, grad_decay, grad_b_matrix, grad_c_matrix)


def solution(mesh):
    placed = (
        P("seq", "head"),
        P("seq", "head"),
        P("seq", "head"),
        P("seq", "head", None),
        P("seq", "head", None),
        P("head"),
        P("seq", "head"),
    )
    return jax.shard_map(
        device_body,
        mesh=mesh,
        in_specs=placed,
        out_specs=(
            P("seq", "head"),
            P("seq", "head"),
            P("seq", "head"),
            P("seq", "head"),
            P("seq", "head", None),
            P("seq", "head", None),
        ),
        check_vma=False,
    )
```

```python
import jax
import jax.numpy as jnp
from jax import lax
from jax.sharding import PartitionSpec as P


SPAN = 128


PRECISION = lax.Precision.HIGH
EPSILON = 1e-05


ROW = 4


def gap_weights(log_carry, place, later, ids=None):
    if ids is None:
        ids = jnp.arange(log_carry.shape[0])
    if later:
        source_ok = ids > place
        between = (ids[None, :] > place) & (ids[None, :] < ids[:, None])
    else:
        source_ok = ids < place
        between = (ids[None, :] > ids[:, None]) & (ids[None, :] < place)
    log_gap = jnp.sum(jnp.where(between[:, :, None, None], log_carry[None], 0.0), axis=1)
    return jnp.where(source_ok[:, None, None], jnp.exp(log_gap), 0.0)


def tile_logs(log_carry, like):
    return jnp.broadcast_to(log_carry[..., None, None], like.shape[:2] + (8, like.shape[3]))


def grouped_gather(value, groups, place):
    size = len(groups[0])
    parts = [value]
    for shift in range(1, size):
        pairs = [(g[k], g[(k + shift) % size]) for g in groups for k in range(size)]
        parts.append(lax.ppermute(value, "seq", pairs))
    sources = (place - jnp.arange(size)) % size
    return jnp.stack(parts), sources


def seq_groups():
    count = lax.axis_size("seq")
    rows = count // ROW
    row_groups = [[z * ROW + x for x in range(ROW)] for z in range(rows)]
    col_groups = [[z * ROW + x for z in range(rows)] for x in range(ROW)]
    return row_groups, col_groups


def prefix_state(final, log_carry):
    place = lax.axis_index("seq")
    col, row = place % ROW, place // ROW
    row_groups, col_groups = seq_groups()
    size = final.shape[2]
    row_all, row_ids = grouped_gather(
        jnp.concatenate([final, tile_logs(log_carry, final)], axis=2), row_groups, col
    )
    row_logs = jnp.max(row_all[:, :, :, size:], axis=(3, 4))
    in_row = weighted_sum(gap_weights(row_logs, col, False, row_ids), row_all)[:, :, :size]
    row_total = weighted_sum(gap_weights(row_logs, ROW, False, row_ids), row_all)[:, :, :size]
    row_log = jnp.sum(row_logs, axis=0)
    col_all, col_ids = grouped_gather(
        jnp.concatenate([row_total, tile_logs(row_log, final)], axis=2), col_groups, row
    )
    col_logs = jnp.max(col_all[:, :, :, size:], axis=(3, 4))
    before_row = weighted_sum(gap_weights(col_logs, row, False, col_ids), col_all)[:, :, :size]
    into_row = jnp.sum(jnp.where((row_ids < col)[:, None, None], row_logs, 0.0), axis=0)
    incoming = in_row + jnp.exp(into_row)[..., None, None] * before_row
    return incoming, (row_logs, row_ids, col_logs, col_ids)


def suffix_state(leaving, logs):
    row_logs, row_ids, col_logs, col_ids = logs
    place = lax.axis_index("seq")
    col, row = place % ROW, place // ROW
    row_groups, col_groups = seq_groups()
    row_all = grouped_gather(leaving, row_groups, col)[0]
    in_row = weighted_sum(gap_weights(row_logs, col, True, row_ids), row_all)
    row_head = weighted_sum(gap_weights(row_logs, -1, True, row_ids), row_all)
    col_all = grouped_gather(row_head, col_groups, row)[0]
    after_row = weighted_sum(gap_weights(col_logs, row, True, col_ids), col_all)
    out_of_row = jnp.sum(jnp.where((row_ids > col)[:, None, None], row_logs, 0.0), axis=0)
    return in_row + jnp.exp(out_of_row)[..., None, None] * after_row


def weighted_sum(weights, states):
    total = weights[0][..., None, None] * states[0]
    for source in range(1, states.shape[0]):
        total = total + weights[source][..., None, None] * states[source]
    return total


def pair_scores(c_half, b_half):
    return jnp.einsum("kign,kjgn->kgij", c_half, b_half, preferred_element_type=jnp.float32)


def score_grads(grad_scores, b_blocks, c_blocks):
    grad_c = jnp.einsum("kgij,kjgn->kign", grad_scores, b_blocks, precision=PRECISION)
    grad_b = jnp.einsum("kgij,kign->kjgn", grad_scores, c_blocks, precision=PRECISION)
    return (grad_b, grad_c)


def block_chain(x_blocks, a_blocks, b_blocks):
    running = jnp.cumsum(jnp.moveaxis(a_blocks, 1, 3), axis=3)
    span_end = running[..., -1]
    to_end = jnp.exp(span_end[..., None] - running)
    scaled = x_blocks * jnp.moveaxis(to_end, 3, 1)[..., None]
    block_states = jnp.einsum("kjgrp,kjgn->kgrpn", scaled, b_blocks, precision=PRECISION)
    factors = jnp.exp(span_end)
    carried = jnp.zeros(block_states.shape[1:], jnp.float32)
    start_list = []
    for block in range(block_states.shape[0]):
        start_list.append(carried)
        carried = factors[block][..., None, None] * carried + block_states[block]
    return (running, span_end, jnp.stack(start_list), carried)


def local_core(x_blocks, a_blocks, b_blocks, c_blocks, scores):
    running, span_end, starts, _ = block_chain(x_blocks, a_blocks, b_blocks)
    length = running.shape[3]
    row_numbers = lax.broadcasted_iota(jnp.int32, (length, length), 0)
    col_ids = lax.broadcasted_iota(jnp.int32, (length, length), 1)
    causal = row_numbers >= col_ids
    log_gaps = running[..., :, None] - running[..., None, :]
    decays = jnp.exp(jnp.where(causal, log_gaps, -1e30))
    weighted = decays * scores[:, :, None]
    diagonal = jnp.einsum("kgrij,kjgrp->kigrp", weighted, x_blocks, precision=PRECISION)
    from_state = jnp.einsum("kign,kgrpn->kigrp", c_blocks, starts, precision=PRECISION)
    ssd_part = diagonal + from_state * jnp.moveaxis(jnp.exp(running), 3, 1)[..., None]
    earlier = jnp.cumsum(span_end, axis=0) - span_end
    reach = jnp.exp(running + earlier[..., None])
    return (ssd_part, reach)


def edge_grads(adjoint, carry_grad, x_blocks, b_blocks, to_end, later, carry_all):
    tokens = x_blocks.shape[0] * x_blocks.shape[1]
    x_tok = x_blocks.reshape((tokens,) + x_blocks.shape[2:])
    b_tok = b_blocks.reshape((tokens,) + b_blocks.shape[2:])
    weights = jnp.exp(jnp.moveaxis(to_end + later[..., None], 3, 1))
    weights = weights.reshape((tokens,) + weights.shape[2:])
    projected = jnp.einsum("tgn,grpn->tgrp", b_tok, adjoint, precision=PRECISION)
    grad_x = weights[..., None] * projected
    log_grad = weights * jnp.sum(x_tok * projected, axis=3)
    grad_b = jnp.einsum("tgrp,grpn->tgn", weights[..., None] * x_tok, adjoint, precision=PRECISION)
    grad_a = jnp.cumsum(log_grad, axis=0) - log_grad + (carry_grad * carry_all)[None]
    return (
        grad_x.reshape(x_blocks.shape),
        grad_a.reshape(x_blocks.shape[:4]),
        grad_b.reshape(b_blocks.shape),
    )


def add_incoming(ssd_part, reach, c_blocks, incoming):
    projected = jnp.einsum("kign,grpn->kigrp", c_blocks, incoming, precision=PRECISION)
    return ssd_part + projected * jnp.moveaxis(reach, 3, 1)[..., None]


def device_body(inputs, gate_input, log_decay, b_matrix, c_matrix, norm_gain, cotangent):
    tok_rows, width = inputs.shape
    head_count = log_decay.shape[1]
    groups = b_matrix.shape[1]
    state_size = b_matrix.shape[2]
    head_size = width // head_count
    per_group = head_count // groups
    blocks = tok_rows // SPAN
    full_width = width * lax.axis_size("head")
    x_blocks = inputs.astype(jnp.float32).reshape(blocks, SPAN, groups, per_group, head_size)
    a_blocks = log_decay.reshape(blocks, SPAN, groups, per_group)
    b_half = b_matrix.reshape(blocks, SPAN, groups, state_size)
    c_half = c_matrix.reshape(blocks, SPAN, groups, state_size)
    b_blocks = b_half.astype(jnp.float32)
    c_blocks = c_half.astype(jnp.float32)
    scores = pair_scores(c_half, b_half)
    core_out, core_pull = jax.vjp(local_core, x_blocks, a_blocks, b_blocks, c_blocks, scores)
    ssd_part, reach = core_out
    ssd_part = lax.optimization_barrier(ssd_part)
    running, span_end, _, final = block_chain(x_blocks, a_blocks, b_blocks)
    carry_all = jnp.exp(jnp.sum(span_end, axis=0))
    to_end = span_end[..., None] - running
    later = jnp.cumsum(span_end[::-1], axis=0)[::-1] - span_end
    log_carry = jnp.sum(a_blocks, axis=(0, 1))
    incoming, seq_logs = prefix_state(final, log_carry)

    def light_step(part_a, part_b, part_c):
        return add_incoming(part_a, part_b, part_c, incoming)

    light_out, light_pull = jax.vjp(light_step, ssd_part, reach, c_blocks)
    ssd_out = light_out.reshape(tok_rows, width)
    gate_value = gate_input.astype(jnp.float32)
    sigmoid_gate = jax.nn.sigmoid(gate_value)
    gate_silu = gate_value * sigmoid_gate
    scaled_cot = norm_gain[None, :] * cotangent.astype(jnp.float32)
    gated = ssd_out * gate_silu
    squares, products = lax.psum(
        (jnp.sum(gated * gated, axis=1), jnp.sum(gated * scaled_cot, axis=1)), "head"
    )
    inverse_rms = lax.rsqrt(squares / full_width + EPSILON)
    normed = (gated * inverse_rms[:, None] * norm_gain[None, :]).astype(jnp.bfloat16)
    grad_gated = (
        inverse_rms[:, None] * scaled_cot
        - gated * (inverse_rms**3 * products / full_width)[:, None]
    )
    grad_gate = (
        grad_gated * ssd_out * sigmoid_gate * (1.0 + gate_value * (1.0 - sigmoid_gate))
    ).astype(jnp.bfloat16)
    grad_ssd = grad_gated * gate_silu
    upstream = grad_ssd.reshape(blocks, SPAN, groups, per_group, head_size)
    reached = upstream * jnp.moveaxis(reach, 3, 1)[..., None]
    leaving = jnp.einsum("kign,kigrp->grpn", c_blocks, reached, precision=PRECISION)
    adjoint = suffix_state(leaving, seq_logs)
    light_grads = light_pull(upstream)
    core_grads = lax.optimization_barrier(core_pull(tuple(light_grads[:2])))
    carry_grad = jnp.sum(adjoint * incoming, axis=(2, 3))
    edge_x, edge_a, edge_b = edge_grads(
        adjoint, carry_grad, x_blocks, b_blocks, to_end, later, carry_all
    )
    grad_x_core, grad_a_core, grad_b_core, grad_c_core, grad_scores = core_grads
    extra_b, extra_c = score_grads(grad_scores, b_blocks, c_blocks)
    grad_x = grad_x_core + edge_x
    grad_a = grad_a_core + edge_a
    grad_b = grad_b_core + extra_b + edge_b
    grad_c = grad_c_core + extra_c + light_grads[2]
    grad_inputs = grad_x.reshape(tok_rows, width).astype(jnp.bfloat16)
    grad_decay = grad_a.reshape(tok_rows, head_count)
    grad_b_matrix = grad_b.reshape(tok_rows, groups, state_size)
    grad_c_matrix = grad_c.reshape(tok_rows, groups, state_size)
    return (normed, grad_inputs, grad_gate, grad_decay, grad_b_matrix, grad_c_matrix)


def solution(mesh):
    placed = (
        P("seq", "head"),
        P("seq", "head"),
        P("seq", "head"),
        P("seq", "head", None),
        P("seq", "head", None),
        P("head"),
        P("seq", "head"),
    )
    return jax.shard_map(
        device_body,
        mesh=mesh,
        in_specs=placed,
        out_specs=(
            P("seq", "head"),
            P("seq", "head"),
            P("seq", "head"),
            P("seq", "head"),
            P("seq", "head", None),
            P("seq", "head", None),
        ),
        check_vma=False,
    )
```

```python
import jax
import jax.numpy as jnp
from jax import lax
from jax.sharding import PartitionSpec as P


SPAN = 128


PRECISION = lax.Precision.HIGH
EXACT = lax.Precision.HIGHEST
EPSILON = 1e-05


ROW = 4


def gap_weights(log_carry, place, later, ids=None):
    if ids is None:
        ids = jnp.arange(log_carry.shape[0])
    if later:
        source_ok = ids > place
        between = (ids[None, :] > place) & (ids[None, :] < ids[:, None])
    else:
        source_ok = ids < place
        between = (ids[None, :] > ids[:, None]) & (ids[None, :] < place)
    log_gap = jnp.sum(jnp.where(between[:, :, None, None], log_carry[None], 0.0), axis=1)
    return jnp.where(source_ok[:, None, None], jnp.exp(log_gap), 0.0)


def tile_logs(log_carry, like):
    return jnp.broadcast_to(log_carry[..., None, None], like.shape[:2] + (8, like.shape[3]))


def grouped_gather(value, groups, place):
    size = len(groups[0])
    parts = [value]
    for shift in range(1, size):
        pairs = [(g[k], g[(k + shift) % size]) for g in groups for k in range(size)]
        parts.append(lax.ppermute(value, "seq", pairs))
    sources = (place - jnp.arange(size)) % size
    return jnp.stack(parts), sources


def seq_groups():
    count = lax.axis_size("seq")
    rows = count // ROW
    row_groups = [[z * ROW + x for x in range(ROW)] for z in range(rows)]
    col_groups = [[z * ROW + x for z in range(rows)] for x in range(ROW)]
    return row_groups, col_groups


def prefix_state(final, log_carry):
    place = lax.axis_index("seq")
    col, row = place % ROW, place // ROW
    row_groups, col_groups = seq_groups()
    size = final.shape[2]
    row_all, row_ids = grouped_gather(
        jnp.concatenate([final, tile_logs(log_carry, final)], axis=2), row_groups, col
    )
    row_logs = jnp.max(row_all[:, :, :, size:], axis=(3, 4))
    in_row = weighted_sum(gap_weights(row_logs, col, False, row_ids), row_all)[:, :, :size]
    row_total = weighted_sum(gap_weights(row_logs, ROW, False, row_ids), row_all)[:, :, :size]
    row_log = jnp.sum(row_logs, axis=0)
    col_all, col_ids = grouped_gather(
        jnp.concatenate([row_total, tile_logs(row_log, final)], axis=2), col_groups, row
    )
    col_logs = jnp.max(col_all[:, :, :, size:], axis=(3, 4))
    before_row = weighted_sum(gap_weights(col_logs, row, False, col_ids), col_all)[:, :, :size]
    into_row = jnp.sum(jnp.where((row_ids < col)[:, None, None], row_logs, 0.0), axis=0)
    incoming = in_row + jnp.exp(into_row)[..., None, None] * before_row
    return incoming, (row_logs, row_ids, col_logs, col_ids)


def suffix_state(leaving, logs):
    row_logs, row_ids, col_logs, col_ids = logs
    place = lax.axis_index("seq")
    col, row = place % ROW, place // ROW
    row_groups, col_groups = seq_groups()
    row_all = grouped_gather(leaving, row_groups, col)[0]
    in_row = weighted_sum(gap_weights(row_logs, col, True, row_ids), row_all)
    row_head = weighted_sum(gap_weights(row_logs, -1, True, row_ids), row_all)
    col_all = grouped_gather(row_head, col_groups, row)[0]
    after_row = weighted_sum(gap_weights(col_logs, row, True, col_ids), col_all)
    out_of_row = jnp.sum(jnp.where((row_ids > col)[:, None, None], row_logs, 0.0), axis=0)
    return in_row + jnp.exp(out_of_row)[..., None, None] * after_row


def weighted_sum(weights, states):
    total = weights[0][..., None, None] * states[0]
    for source in range(1, states.shape[0]):
        total = total + weights[source][..., None, None] * states[source]
    return total


def pair_scores(c_half, b_half):
    return jnp.einsum("kign,kjgn->kgij", c_half, b_half, preferred_element_type=jnp.float32)


def score_grads(grad_scores, b_blocks, c_blocks):
    grad_c = jnp.einsum("kgij,kjgn->kign", grad_scores, b_blocks, precision=PRECISION)
    grad_b = jnp.einsum("kgij,kign->kjgn", grad_scores, c_blocks, precision=PRECISION)
    return (grad_b, grad_c)


def block_chain(x_blocks, a_blocks, b_blocks):
    length = a_blocks.shape[1]
    ids = jnp.arange(length)
    lower = (ids[:, None] >= ids[None, :]).astype(jnp.float32)
    running = jnp.einsum("kjgr,ij->kgri", a_blocks, lower, precision=EXACT)
    span_end = running[..., -1]
    to_end = jnp.exp(span_end[..., None] - running)
    scaled = x_blocks * jnp.moveaxis(to_end, 3, 1)[..., None]
    block_states = jnp.einsum("kjgrp,kjgn->kgrpn", scaled, b_blocks, precision=PRECISION)
    factors = jnp.exp(span_end)
    carried = jnp.zeros(block_states.shape[1:], jnp.float32)
    start_list = []
    for block in range(block_states.shape[0]):
        start_list.append(carried)
        carried = factors[block][..., None, None] * carried + block_states[block]
    return (running, span_end, jnp.stack(start_list), carried)


def local_core(x_blocks, a_blocks, b_blocks, c_blocks, scores):
    running, span_end, starts, _ = block_chain(x_blocks, a_blocks, b_blocks)
    length = running.shape[3]
    row_numbers = lax.broadcasted_iota(jnp.int32, (length, length), 0)
    col_ids = lax.broadcasted_iota(jnp.int32, (length, length), 1)
    causal = row_numbers >= col_ids
    log_gaps = running[..., :, None] - running[..., None, :]
    decays = jnp.exp(jnp.where(causal, log_gaps, -1e30))
    weighted = decays * scores[:, :, None]
    diagonal = jnp.einsum("kgrij,kjgrp->kigrp", weighted, x_blocks, precision=PRECISION)
    from_state = jnp.einsum("kign,kgrpn->kigrp", c_blocks, starts, precision=PRECISION)
    ssd_part = diagonal + from_state * jnp.moveaxis(jnp.exp(running), 3, 1)[..., None]
    earlier = jnp.cumsum(span_end, axis=0) - span_end
    reach = jnp.exp(running + earlier[..., None])
    return (ssd_part, reach)


def edge_grads(adjoint, carry_grad, x_blocks, b_blocks, to_end, later, carry_all):
    tokens = x_blocks.shape[0] * x_blocks.shape[1]
    x_tok = x_blocks.reshape((tokens,) + x_blocks.shape[2:])
    b_tok = b_blocks.reshape((tokens,) + b_blocks.shape[2:])
    weights = jnp.exp(jnp.moveaxis(to_end + later[..., None], 3, 1))
    weights = weights.reshape((tokens,) + weights.shape[2:])
    projected = jnp.einsum("tgn,grpn->tgrp", b_tok, adjoint, precision=PRECISION)
    grad_x = weights[..., None] * projected
    log_grad = weights * jnp.sum(x_tok * projected, axis=3)
    grad_b = jnp.einsum("tgrp,grpn->tgn", weights[..., None] * x_tok, adjoint, precision=PRECISION)
    ids = jnp.arange(tokens)
    strict = (ids[:, None] > ids[None, :]).astype(jnp.float32)
    before = jnp.einsum("tgr,st->sgr", log_grad, strict, precision=EXACT)
    grad_a = before + (carry_grad * carry_all)[None]
    return (
        grad_x.reshape(x_blocks.shape),
        grad_a.reshape(x_blocks.shape[:4]),
        grad_b.reshape(b_blocks.shape),
    )


def add_incoming(ssd_part, reach, c_blocks, incoming):
    projected = jnp.einsum("kign,grpn->kigrp", c_blocks, incoming, precision=PRECISION)
    return ssd_part + projected * jnp.moveaxis(reach, 3, 1)[..., None]


def device_body(inputs, gate_input, log_decay, b_matrix, c_matrix, norm_gain, cotangent):
    tok_rows, width = inputs.shape
    head_count = log_decay.shape[1]
    groups = b_matrix.shape[1]
    state_size = b_matrix.shape[2]
    head_size = width // head_count
    per_group = head_count // groups
    blocks = tok_rows // SPAN
    full_width = width * lax.axis_size("head")
    x_blocks = inputs.astype(jnp.float32).reshape(blocks, SPAN, groups, per_group, head_size)
    a_blocks = log_decay.reshape(blocks, SPAN, groups, per_group)
    b_half = b_matrix.reshape(blocks, SPAN, groups, state_size)
    c_half = c_matrix.reshape(blocks, SPAN, groups, state_size)
    b_blocks = b_half.astype(jnp.float32)
    c_blocks = c_half.astype(jnp.float32)
    scores = pair_scores(c_half, b_half)
    core_out, core_pull = jax.vjp(local_core, x_blocks, a_blocks, b_blocks, c_blocks, scores)
    ssd_part, reach = core_out
    ssd_part = lax.optimization_barrier(ssd_part)
    running, span_end, _, final = block_chain(x_blocks, a_blocks, b_blocks)
    carry_all = jnp.exp(jnp.sum(span_end, axis=0))
    to_end = span_end[..., None] - running
    later = jnp.cumsum(span_end[::-1], axis=0)[::-1] - span_end
    log_carry = jnp.sum(a_blocks, axis=(0, 1))
    incoming, seq_logs = prefix_state(final, log_carry)

    def light_step(part_a, part_b, part_c):
        return add_incoming(part_a, part_b, part_c, incoming)

    light_out, light_pull = jax.vjp(light_step, ssd_part, reach, c_blocks)
    ssd_out = light_out.reshape(tok_rows, width)
    gate_value = gate_input.astype(jnp.float32)
    sigmoid_gate = jax.nn.sigmoid(gate_value)
    gate_silu = gate_value * sigmoid_gate
    scaled_cot = norm_gain[None, :] * cotangent.astype(jnp.float32)
    gated = ssd_out * gate_silu
    squares, products = lax.psum(
        (jnp.sum(gated * gated, axis=1), jnp.sum(gated * scaled_cot, axis=1)), "head"
    )
    inverse_rms = lax.rsqrt(squares / full_width + EPSILON)
    normed = (gated * inverse_rms[:, None] * norm_gain[None, :]).astype(jnp.bfloat16)
    grad_gated = (
        inverse_rms[:, None] * scaled_cot
        - gated * (inverse_rms**3 * products / full_width)[:, None]
    )
    grad_gate = (
        grad_gated * ssd_out * sigmoid_gate * (1.0 + gate_value * (1.0 - sigmoid_gate))
    ).astype(jnp.bfloat16)
    grad_ssd = grad_gated * gate_silu
    upstream = grad_ssd.reshape(blocks, SPAN, groups, per_group, head_size)
    reached = upstream * jnp.moveaxis(reach, 3, 1)[..., None]
    leaving = jnp.einsum("kign,kigrp->grpn", c_blocks, reached, precision=PRECISION)
    adjoint = suffix_state(leaving, seq_logs)
    light_grads = light_pull(upstream)
    core_grads = lax.optimization_barrier(core_pull(tuple(light_grads[:2])))
    carry_grad = jnp.sum(adjoint * incoming, axis=(2, 3))
    edge_x, edge_a, edge_b = edge_grads(
        adjoint, carry_grad, x_blocks, b_blocks, to_end, later, carry_all
    )
    grad_x_core, grad_a_core, grad_b_core, grad_c_core, grad_scores = core_grads
    extra_b, extra_c = score_grads(grad_scores, b_blocks, c_blocks)
    grad_x = grad_x_core + edge_x
    grad_a = grad_a_core + edge_a
    grad_b = grad_b_core + extra_b + edge_b
    grad_c = grad_c_core + extra_c + light_grads[2]
    grad_inputs = grad_x.reshape(tok_rows, width).astype(jnp.bfloat16)
    grad_decay = grad_a.reshape(tok_rows, head_count)
    grad_b_matrix = grad_b.reshape(tok_rows, groups, state_size)
    grad_c_matrix = grad_c.reshape(tok_rows, groups, state_size)
    return (normed, grad_inputs, grad_gate, grad_decay, grad_b_matrix, grad_c_matrix)


def solution(mesh):
    placed = (
        P("seq", "head"),
        P("seq", "head"),
        P("seq", "head"),
        P("seq", "head", None),
        P("seq", "head", None),
        P("head"),
        P("seq", "head"),
    )
    return jax.shard_map(
        device_body,
        mesh=mesh,
        in_specs=placed,
        out_specs=(
            P("seq", "head"),
            P("seq", "head"),
            P("seq", "head"),
            P("seq", "head"),
            P("seq", "head", None),
            P("seq", "head", None),
        ),
        check_vma=False,
    )
```

```python
import jax
import jax.numpy as jnp
from jax import lax
from jax.sharding import PartitionSpec as P


SPAN = 128


PRECISION = lax.Precision.HIGH
EXACT = lax.Precision.HIGHEST
EPSILON = 1e-05


ROW = 4


def gap_weights(log_carry, place, later, ids=None):
    if ids is None:
        ids = jnp.arange(log_carry.shape[0])
    if later:
        source_ok = ids > place
        between = (ids[None, :] > place) & (ids[None, :] < ids[:, None])
    else:
        source_ok = ids < place
        between = (ids[None, :] > ids[:, None]) & (ids[None, :] < place)
    log_gap = jnp.sum(jnp.where(between[:, :, None, None], log_carry[None], 0.0), axis=1)
    return jnp.where(source_ok[:, None, None], jnp.exp(log_gap), 0.0)


def tile_logs(log_carry, like):
    return jnp.broadcast_to(log_carry[..., None, None], like.shape[:2] + (8, like.shape[3]))


def grouped_gather(value, groups, place):
    size = len(groups[0])
    parts = [value]
    for shift in range(1, size):
        pairs = [(g[k], g[(k + shift) % size]) for g in groups for k in range(size)]
        parts.append(lax.ppermute(value, "seq", pairs))
    sources = (place - jnp.arange(size)) % size
    return jnp.stack(parts), sources


def seq_groups():
    count = lax.axis_size("seq")
    rows = count // ROW
    row_groups = [[z * ROW + x for x in range(ROW)] for z in range(rows)]
    col_groups = [[z * ROW + x for z in range(rows)] for x in range(ROW)]
    return row_groups, col_groups


def prefix_state(final, log_carry):
    place = lax.axis_index("seq")
    col, row = place % ROW, place // ROW
    row_groups, col_groups = seq_groups()
    size = final.shape[2]
    row_all, row_ids = grouped_gather(
        jnp.concatenate([final, tile_logs(log_carry, final)], axis=2), row_groups, col
    )
    row_logs = jnp.max(row_all[:, :, :, size:], axis=(3, 4))
    in_row = weighted_sum(gap_weights(row_logs, col, False, row_ids), row_all)[:, :, :size]
    row_total = weighted_sum(gap_weights(row_logs, ROW, False, row_ids), row_all)[:, :, :size]
    row_log = jnp.sum(row_logs, axis=0)
    col_all, col_ids = grouped_gather(
        jnp.concatenate([row_total, tile_logs(row_log, final)], axis=2), col_groups, row
    )
    col_logs = jnp.max(col_all[:, :, :, size:], axis=(3, 4))
    before_row = weighted_sum(gap_weights(col_logs, row, False, col_ids), col_all)[:, :, :size]
    into_row = jnp.sum(jnp.where((row_ids < col)[:, None, None], row_logs, 0.0), axis=0)
    incoming = in_row + jnp.exp(into_row)[..., None, None] * before_row
    return incoming, (row_logs, row_ids, col_logs, col_ids)


def suffix_state(leaving, logs):
    row_logs, row_ids, col_logs, col_ids = logs
    place = lax.axis_index("seq")
    col, row = place % ROW, place // ROW
    row_groups, col_groups = seq_groups()
    row_all = grouped_gather(leaving, row_groups, col)[0]
    in_row = weighted_sum(gap_weights(row_logs, col, True, row_ids), row_all)
    row_head = weighted_sum(gap_weights(row_logs, -1, True, row_ids), row_all)
    col_all = grouped_gather(row_head, col_groups, row)[0]
    after_row = weighted_sum(gap_weights(col_logs, row, True, col_ids), col_all)
    out_of_row = jnp.sum(jnp.where((row_ids > col)[:, None, None], row_logs, 0.0), axis=0)
    return in_row + jnp.exp(out_of_row)[..., None, None] * after_row


def head_sum(values):
    count = lax.axis_size("head")
    if count & (count - 1):
        return lax.psum(values, "head")
    shift = 1
    while shift < count:
        pairs = [(i, i ^ shift) for i in range(count)]
        values = values + lax.ppermute(values, "head", pairs)
        shift *= 2
    return values


def weighted_sum(weights, states):
    total = weights[0][..., None, None] * states[0]
    for source in range(1, states.shape[0]):
        total = total + weights[source][..., None, None] * states[source]
    return total


def pair_scores(c_half, b_half):
    return jnp.einsum("kign,kjgn->kgij", c_half, b_half, preferred_element_type=jnp.float32)


def score_grads(grad_scores, b_blocks, c_blocks):
    grad_c = jnp.einsum("kgij,kjgn->kign", grad_scores, b_blocks, precision=PRECISION)
    grad_b = jnp.einsum("kgij,kign->kjgn", grad_scores, c_blocks, precision=PRECISION)
    return (grad_b, grad_c)


def block_chain(x_blocks, a_blocks, b_blocks):
    length = a_blocks.shape[1]
    ids = jnp.arange(length)
    lower = (ids[:, None] >= ids[None, :]).astype(jnp.float32)
    running = jnp.einsum("kjgr,ij->kgri", a_blocks, lower, precision=EXACT)
    span_end = running[..., -1]
    to_end = jnp.exp(span_end[..., None] - running)
    scaled = x_blocks * jnp.moveaxis(to_end, 3, 1)[..., None]
    block_states = jnp.einsum("kjgrp,kjgn->kgrpn", scaled, b_blocks, precision=PRECISION)
    factors = jnp.exp(span_end)
    carried = jnp.zeros(block_states.shape[1:], jnp.float32)
    start_list = []
    for block in range(block_states.shape[0]):
        start_list.append(carried)
        carried = factors[block][..., None, None] * carried + block_states[block]
    return (running, span_end, jnp.stack(start_list), carried)


def local_core(x_blocks, a_blocks, b_blocks, c_blocks, scores):
    running, span_end, starts, _ = block_chain(x_blocks, a_blocks, b_blocks)
    length = running.shape[3]
    row_numbers = lax.broadcasted_iota(jnp.int32, (length, length), 0)
    col_ids = lax.broadcasted_iota(jnp.int32, (length, length), 1)
    causal = row_numbers >= col_ids
    log_gaps = running[..., :, None] - running[..., None, :]
    decays = jnp.exp(jnp.where(causal, log_gaps, -1e30))
    weighted = decays * scores[:, :, None]
    diagonal = jnp.einsum("kgrij,kjgrp->kigrp", weighted, x_blocks, precision=PRECISION)
    from_state = jnp.einsum("kign,kgrpn->kigrp", c_blocks, starts, precision=PRECISION)
    ssd_part = diagonal + from_state * jnp.moveaxis(jnp.exp(running), 3, 1)[..., None]
    earlier = jnp.cumsum(span_end, axis=0) - span_end
    reach = jnp.exp(running + earlier[..., None])
    return (ssd_part, reach)


def edge_grads(adjoint, carry_grad, x_blocks, b_blocks, to_end, later, carry_all):
    tokens = x_blocks.shape[0] * x_blocks.shape[1]
    x_tok = x_blocks.reshape((tokens,) + x_blocks.shape[2:])
    b_tok = b_blocks.reshape((tokens,) + b_blocks.shape[2:])
    weights = jnp.exp(jnp.moveaxis(to_end + later[..., None], 3, 1))
    weights = weights.reshape((tokens,) + weights.shape[2:])
    projected = jnp.einsum("tgn,grpn->tgrp", b_tok, adjoint, precision=PRECISION)
    grad_x = weights[..., None] * projected
    log_grad = weights * jnp.sum(x_tok * projected, axis=3)
    grad_b = jnp.einsum("tgrp,grpn->tgn", weights[..., None] * x_tok, adjoint, precision=PRECISION)
    ids = jnp.arange(tokens)
    strict = (ids[:, None] > ids[None, :]).astype(jnp.float32)
    before = jnp.einsum("tgr,st->sgr", log_grad, strict, precision=EXACT)
    grad_a = before + (carry_grad * carry_all)[None]
    return (
        grad_x.reshape(x_blocks.shape),
        grad_a.reshape(x_blocks.shape[:4]),
        grad_b.reshape(b_blocks.shape),
    )


def add_incoming(ssd_part, reach, c_blocks, incoming):
    projected = jnp.einsum("kign,grpn->kigrp", c_blocks, incoming, precision=PRECISION)
    return ssd_part + projected * jnp.moveaxis(reach, 3, 1)[..., None]


def device_body(inputs, gate_input, log_decay, b_matrix, c_matrix, norm_gain, cotangent):
    tok_rows, width = inputs.shape
    head_count = log_decay.shape[1]
    groups = b_matrix.shape[1]
    state_size = b_matrix.shape[2]
    head_size = width // head_count
    per_group = head_count // groups
    blocks = tok_rows // SPAN
    full_width = width * lax.axis_size("head")
    x_blocks = inputs.astype(jnp.float32).reshape(blocks, SPAN, groups, per_group, head_size)
    a_blocks = log_decay.reshape(blocks, SPAN, groups, per_group)
    b_half = b_matrix.reshape(blocks, SPAN, groups, state_size)
    c_half = c_matrix.reshape(blocks, SPAN, groups, state_size)
    b_blocks = b_half.astype(jnp.float32)
    c_blocks = c_half.astype(jnp.float32)
    scores = pair_scores(c_half, b_half)
    core_out, core_pull = jax.vjp(local_core, x_blocks, a_blocks, b_blocks, c_blocks, scores)
    ssd_part, reach = core_out
    ssd_part = lax.optimization_barrier(ssd_part)
    running, span_end, _, final = block_chain(x_blocks, a_blocks, b_blocks)
    carry_all = jnp.exp(jnp.sum(span_end, axis=0))
    to_end = span_end[..., None] - running
    later = jnp.cumsum(span_end[::-1], axis=0)[::-1] - span_end
    log_carry = jnp.sum(a_blocks, axis=(0, 1))
    incoming, seq_logs = prefix_state(final, log_carry)

    def light_step(part_a, part_b, part_c):
        return add_incoming(part_a, part_b, part_c, incoming)

    light_out, light_pull = jax.vjp(light_step, ssd_part, reach, c_blocks)
    ssd_out = light_out.reshape(tok_rows, width)
    gate_value = gate_input.astype(jnp.float32)
    sigmoid_gate = jax.nn.sigmoid(gate_value)
    gate_silu = gate_value * sigmoid_gate
    scaled_cot = norm_gain[None, :] * cotangent.astype(jnp.float32)
    gated = ssd_out * gate_silu
    squares, products = head_sum(
        jnp.stack([jnp.sum(gated * gated, axis=1), jnp.sum(gated * scaled_cot, axis=1)])
    )
    inverse_rms = lax.rsqrt(squares / full_width + EPSILON)
    normed = (gated * inverse_rms[:, None] * norm_gain[None, :]).astype(jnp.bfloat16)
    grad_gated = (
        inverse_rms[:, None] * scaled_cot
        - gated * (inverse_rms**3 * products / full_width)[:, None]
    )
    grad_gate = (
        grad_gated * ssd_out * sigmoid_gate * (1.0 + gate_value * (1.0 - sigmoid_gate))
    ).astype(jnp.bfloat16)
    grad_ssd = grad_gated * gate_silu
    upstream = grad_ssd.reshape(blocks, SPAN, groups, per_group, head_size)
    reached = upstream * jnp.moveaxis(reach, 3, 1)[..., None]
    leaving = jnp.einsum("kign,kigrp->grpn", c_blocks, reached, precision=PRECISION)
    adjoint = suffix_state(leaving, seq_logs)
    light_grads = light_pull(upstream)
    core_grads = lax.optimization_barrier(core_pull(tuple(light_grads[:2])))
    carry_grad = jnp.sum(adjoint * incoming, axis=(2, 3))
    edge_x, edge_a, edge_b = edge_grads(
        adjoint, carry_grad, x_blocks, b_blocks, to_end, later, carry_all
    )
    grad_x_core, grad_a_core, grad_b_core, grad_c_core, grad_scores = core_grads
    extra_b, extra_c = score_grads(grad_scores, b_blocks, c_blocks)
    grad_x = grad_x_core + edge_x
    grad_a = grad_a_core + edge_a
    grad_b = grad_b_core + extra_b + edge_b
    grad_c = grad_c_core + extra_c + light_grads[2]
    grad_inputs = grad_x.reshape(tok_rows, width).astype(jnp.bfloat16)
    grad_decay = grad_a.reshape(tok_rows, head_count)
    grad_b_matrix = grad_b.reshape(tok_rows, groups, state_size)
    grad_c_matrix = grad_c.reshape(tok_rows, groups, state_size)
    return (normed, grad_inputs, grad_gate, grad_decay, grad_b_matrix, grad_c_matrix)


def solution(mesh):
    placed = (
        P("seq", "head"),
        P("seq", "head"),
        P("seq", "head"),
        P("seq", "head", None),
        P("seq", "head", None),
        P("head"),
        P("seq", "head"),
    )
    return jax.shard_map(
        device_body,
        mesh=mesh,
        in_specs=placed,
        out_specs=(
            P("seq", "head"),
            P("seq", "head"),
            P("seq", "head"),
            P("seq", "head"),
            P("seq", "head", None),
            P("seq", "head", None),
        ),
        check_vma=False,
    )
```

```python
import jax
import jax.numpy as jnp
from jax import lax
from jax.sharding import PartitionSpec as P


SPAN = 128


PRECISION = lax.Precision.HIGH
EXACT = lax.Precision.HIGHEST
EPSILON = 1e-05


ROW = 4


def gap_weights(log_carry, place, later, ids=None):
    if ids is None:
        ids = jnp.arange(log_carry.shape[0])
    if later:
        source_ok = ids > place
        between = (ids[None, :] > place) & (ids[None, :] < ids[:, None])
    else:
        source_ok = ids < place
        between = (ids[None, :] > ids[:, None]) & (ids[None, :] < place)
    log_gap = jnp.sum(jnp.where(between[:, :, None, None], log_carry[None], 0.0), axis=1)
    return jnp.where(source_ok[:, None, None], jnp.exp(log_gap), 0.0)


def tile_logs(log_carry, like):
    return jnp.broadcast_to(log_carry[..., None, None], like.shape[:2] + (8, like.shape[3]))


def grouped_gather(value, groups, place):
    size = len(groups[0])
    parts = [value]
    for shift in range(1, size):
        pairs = [(g[k], g[(k + shift) % size]) for g in groups for k in range(size)]
        parts.append(lax.ppermute(value, "seq", pairs))
    sources = (place - jnp.arange(size)) % size
    return jnp.stack(parts), sources


def seq_groups():
    count = lax.axis_size("seq")
    rows = count // ROW
    row_groups = [[z * ROW + x for x in range(ROW)] for z in range(rows)]
    col_groups = [[z * ROW + x for z in range(rows)] for x in range(ROW)]
    return row_groups, col_groups


def prefix_rows(final, log_carry):
    place = lax.axis_index("seq")
    col = place % ROW
    row_groups, _ = seq_groups()
    size = final.shape[2]
    row_all, row_ids = grouped_gather(
        jnp.concatenate([final, tile_logs(log_carry, final)], axis=2), row_groups, col
    )
    row_logs = jnp.max(row_all[:, :, :, size:], axis=(3, 4))
    in_row = weighted_sum(gap_weights(row_logs, col, False, row_ids), row_all)[:, :, :size]
    row_total = weighted_sum(gap_weights(row_logs, ROW, False, row_ids), row_all)[:, :, :size]
    row_log = jnp.sum(row_logs, axis=0)
    payload = jnp.concatenate([row_total, tile_logs(row_log, final)], axis=2)
    return payload, (in_row, row_logs, row_ids)


def prefix_cols(payload, row_part):
    in_row, row_logs, row_ids = row_part
    place = lax.axis_index("seq")
    col, row = place % ROW, place // ROW
    _, col_groups = seq_groups()
    size = in_row.shape[2]
    col_all, col_ids = grouped_gather(payload, col_groups, row)
    col_logs = jnp.max(col_all[:, :, :, size:], axis=(3, 4))
    before_row = weighted_sum(gap_weights(col_logs, row, False, col_ids), col_all)[:, :, :size]
    into_row = jnp.sum(jnp.where((row_ids < col)[:, None, None], row_logs, 0.0), axis=0)
    incoming = in_row + jnp.exp(into_row)[..., None, None] * before_row
    return incoming, (row_logs, row_ids, col_logs, col_ids)


def suffix_state(leaving, logs):
    row_logs, row_ids, col_logs, col_ids = logs
    place = lax.axis_index("seq")
    col, row = place % ROW, place // ROW
    row_groups, col_groups = seq_groups()
    row_all = grouped_gather(leaving, row_groups, col)[0]
    in_row = weighted_sum(gap_weights(row_logs, col, True, row_ids), row_all)
    row_head = weighted_sum(gap_weights(row_logs, -1, True, row_ids), row_all)
    col_all = grouped_gather(row_head, col_groups, row)[0]
    after_row = weighted_sum(gap_weights(col_logs, row, True, col_ids), col_all)
    out_of_row = jnp.sum(jnp.where((row_ids > col)[:, None, None], row_logs, 0.0), axis=0)
    return in_row + jnp.exp(out_of_row)[..., None, None] * after_row


def head_sum(values):
    count = lax.axis_size("head")
    if count & (count - 1):
        return lax.psum(values, "head")
    shift = 1
    while shift < count:
        pairs = [(i, i ^ shift) for i in range(count)]
        values = values + lax.ppermute(values, "head", pairs)
        shift *= 2
    return values


def weighted_sum(weights, states):
    total = weights[0][..., None, None] * states[0]
    for source in range(1, states.shape[0]):
        total = total + weights[source][..., None, None] * states[source]
    return total


def pair_scores(c_half, b_half):
    return jnp.einsum("kign,kjgn->kgij", c_half, b_half, preferred_element_type=jnp.float32)


def score_grads(grad_scores, b_blocks, c_blocks):
    grad_c = jnp.einsum("kgij,kjgn->kign", grad_scores, b_blocks, precision=PRECISION)
    grad_b = jnp.einsum("kgij,kign->kjgn", grad_scores, c_blocks, precision=PRECISION)
    return (grad_b, grad_c)


def block_chain(x_blocks, a_blocks, b_blocks):
    length = a_blocks.shape[1]
    ids = jnp.arange(length)
    lower = (ids[:, None] >= ids[None, :]).astype(jnp.float32)
    running = jnp.einsum("kjgr,ij->kgri", a_blocks, lower, precision=EXACT)
    span_end = running[..., -1]
    to_end = jnp.exp(span_end[..., None] - running)
    scaled = x_blocks * jnp.moveaxis(to_end, 3, 1)[..., None]
    block_states = jnp.einsum("kjgrp,kjgn->kgrpn", scaled, b_blocks, precision=PRECISION)
    factors = jnp.exp(span_end)
    carried = jnp.zeros(block_states.shape[1:], jnp.float32)
    start_list = []
    for block in range(block_states.shape[0]):
        start_list.append(carried)
        carried = factors[block][..., None, None] * carried + block_states[block]
    return (running, span_end, jnp.stack(start_list), carried)


def local_core(x_blocks, a_blocks, b_blocks, c_blocks, scores):
    running, span_end, starts, _ = block_chain(x_blocks, a_blocks, b_blocks)
    length = running.shape[3]
    row_numbers = lax.broadcasted_iota(jnp.int32, (length, length), 0)
    col_ids = lax.broadcasted_iota(jnp.int32, (length, length), 1)
    causal = row_numbers >= col_ids
    log_gaps = running[..., :, None] - running[..., None, :]
    decays = jnp.exp(jnp.where(causal, log_gaps, -1e30))
    weighted = decays * scores[:, :, None]
    diagonal = jnp.einsum("kgrij,kjgrp->kigrp", weighted, x_blocks, precision=PRECISION)
    from_state = jnp.einsum("kign,kgrpn->kigrp", c_blocks, starts, precision=PRECISION)
    ssd_part = diagonal + from_state * jnp.moveaxis(jnp.exp(running), 3, 1)[..., None]
    earlier = jnp.cumsum(span_end, axis=0) - span_end
    reach = jnp.exp(running + earlier[..., None])
    return (ssd_part, reach)


def edge_grads(adjoint, carry_grad, x_blocks, b_blocks, to_end, later, carry_all):
    tokens = x_blocks.shape[0] * x_blocks.shape[1]
    x_tok = x_blocks.reshape((tokens,) + x_blocks.shape[2:])
    b_tok = b_blocks.reshape((tokens,) + b_blocks.shape[2:])
    weights = jnp.exp(jnp.moveaxis(to_end + later[..., None], 3, 1))
    weights = weights.reshape((tokens,) + weights.shape[2:])
    projected = jnp.einsum("tgn,grpn->tgrp", b_tok, adjoint, precision=PRECISION)
    grad_x = weights[..., None] * projected
    log_grad = weights * jnp.sum(x_tok * projected, axis=3)
    grad_b = jnp.einsum("tgrp,grpn->tgn", weights[..., None] * x_tok, adjoint, precision=PRECISION)
    ids = jnp.arange(tokens)
    strict = (ids[:, None] > ids[None, :]).astype(jnp.float32)
    before = jnp.einsum("tgr,st->sgr", log_grad, strict, precision=EXACT)
    grad_a = before + (carry_grad * carry_all)[None]
    return (
        grad_x.reshape(x_blocks.shape),
        grad_a.reshape(x_blocks.shape[:4]),
        grad_b.reshape(b_blocks.shape),
    )


def add_incoming(ssd_part, reach, c_blocks, incoming):
    projected = jnp.einsum("kign,grpn->kigrp", c_blocks, incoming, precision=PRECISION)
    return ssd_part + projected * jnp.moveaxis(reach, 3, 1)[..., None]


def device_body(inputs, gate_input, log_decay, b_matrix, c_matrix, norm_gain, cotangent):
    tok_rows, width = inputs.shape
    head_count = log_decay.shape[1]
    groups = b_matrix.shape[1]
    state_size = b_matrix.shape[2]
    head_size = width // head_count
    per_group = head_count // groups
    blocks = tok_rows // SPAN
    full_width = width * lax.axis_size("head")
    x_blocks = inputs.astype(jnp.float32).reshape(blocks, SPAN, groups, per_group, head_size)
    a_blocks = log_decay.reshape(blocks, SPAN, groups, per_group)
    b_half = b_matrix.reshape(blocks, SPAN, groups, state_size)
    c_half = c_matrix.reshape(blocks, SPAN, groups, state_size)
    b_blocks = b_half.astype(jnp.float32)
    c_blocks = c_half.astype(jnp.float32)
    scores = pair_scores(c_half, b_half)
    core_out, core_pull = jax.vjp(local_core, x_blocks, a_blocks, b_blocks, c_blocks, scores)
    ssd_part, reach = core_out
    ssd_part = lax.optimization_barrier(ssd_part)
    running, span_end, _, final = block_chain(x_blocks, a_blocks, b_blocks)
    carry_all = jnp.exp(jnp.sum(span_end, axis=0))
    to_end = span_end[..., None] - running
    later = jnp.cumsum(span_end[::-1], axis=0)[::-1] - span_end
    log_carry = jnp.sum(a_blocks, axis=(0, 1))
    half = final.shape[1] // 2
    payload_a, rows_a = prefix_rows(final[:, :half], log_carry[:, :half])
    payload_a, final_b, log_b = lax.optimization_barrier(
        (payload_a, final[:, half:], log_carry[:, half:])
    )
    payload_b, rows_b = prefix_rows(final_b, log_b)
    incoming_a, logs_a = prefix_cols(payload_a, rows_a)
    incoming_b, logs_b = prefix_cols(payload_b, rows_b)
    incoming = jnp.concatenate([incoming_a, incoming_b], axis=1)

    def light_step(part_a, part_b, part_c):
        return add_incoming(part_a, part_b, part_c, incoming)

    light_out, light_pull = jax.vjp(light_step, ssd_part, reach, c_blocks)
    ssd_out = light_out.reshape(tok_rows, width)
    gate_value = gate_input.astype(jnp.float32)
    sigmoid_gate = jax.nn.sigmoid(gate_value)
    gate_silu = gate_value * sigmoid_gate
    scaled_cot = norm_gain[None, :] * cotangent.astype(jnp.float32)
    gated = ssd_out * gate_silu
    squares, products = head_sum(
        jnp.stack([jnp.sum(gated * gated, axis=1), jnp.sum(gated * scaled_cot, axis=1)])
    )
    inverse_rms = lax.rsqrt(squares / full_width + EPSILON)
    normed = (gated * inverse_rms[:, None] * norm_gain[None, :]).astype(jnp.bfloat16)
    grad_gated = (
        inverse_rms[:, None] * scaled_cot
        - gated * (inverse_rms**3 * products / full_width)[:, None]
    )
    grad_gate = (
        grad_gated * ssd_out * sigmoid_gate * (1.0 + gate_value * (1.0 - sigmoid_gate))
    ).astype(jnp.bfloat16)
    grad_ssd = grad_gated * gate_silu
    upstream = grad_ssd.reshape(blocks, SPAN, groups, per_group, head_size)
    reached = upstream * jnp.moveaxis(reach, 3, 1)[..., None]
    leaving = jnp.einsum("kign,kigrp->grpn", c_blocks, reached, precision=PRECISION)
    adjoint = jnp.concatenate(
        [suffix_state(leaving[:, :half], logs_a), suffix_state(leaving[:, half:], logs_b)],
        axis=1,
    )
    light_grads = light_pull(upstream)
    core_grads = lax.optimization_barrier(core_pull(tuple(light_grads[:2])))
    carry_grad = jnp.sum(adjoint * incoming, axis=(2, 3))
    edge_x, edge_a, edge_b = edge_grads(
        adjoint, carry_grad, x_blocks, b_blocks, to_end, later, carry_all
    )
    grad_x_core, grad_a_core, grad_b_core, grad_c_core, grad_scores = core_grads
    extra_b, extra_c = score_grads(grad_scores, b_blocks, c_blocks)
    grad_x = grad_x_core + edge_x
    grad_a = grad_a_core + edge_a
    grad_b = grad_b_core + extra_b + edge_b
    grad_c = grad_c_core + extra_c + light_grads[2]
    grad_inputs = grad_x.reshape(tok_rows, width).astype(jnp.bfloat16)
    grad_decay = grad_a.reshape(tok_rows, head_count)
    grad_b_matrix = grad_b.reshape(tok_rows, groups, state_size)
    grad_c_matrix = grad_c.reshape(tok_rows, groups, state_size)
    return (normed, grad_inputs, grad_gate, grad_decay, grad_b_matrix, grad_c_matrix)


def solution(mesh):
    placed = (
        P("seq", "head"),
        P("seq", "head"),
        P("seq", "head"),
        P("seq", "head", None),
        P("seq", "head", None),
        P("head"),
        P("seq", "head"),
    )
    return jax.shard_map(
        device_body,
        mesh=mesh,
        in_specs=placed,
        out_specs=(
            P("seq", "head"),
            P("seq", "head"),
            P("seq", "head"),
            P("seq", "head"),
            P("seq", "head", None),
            P("seq", "head", None),
        ),
        check_vma=False,
    )
```

```python
import jax
import jax.numpy as jnp
from jax import lax
from jax.sharding import PartitionSpec as P


SPAN = 128


PRECISION = lax.Precision.HIGH
EXACT = lax.Precision.HIGHEST
EPSILON = 1e-05


ROW = 4


def gap_weights(log_carry, place, later, ids=None):
    if ids is None:
        ids = jnp.arange(log_carry.shape[0])
    if later:
        source_ok = ids > place
        between = (ids[None, :] > place) & (ids[None, :] < ids[:, None])
    else:
        source_ok = ids < place
        between = (ids[None, :] > ids[:, None]) & (ids[None, :] < place)
    log_gap = jnp.sum(jnp.where(between[:, :, None, None], log_carry[None], 0.0), axis=1)
    return jnp.where(source_ok[:, None, None], jnp.exp(log_gap), 0.0)


def tile_logs(log_carry, like):
    return jnp.broadcast_to(log_carry[..., None, None], like.shape[:2] + (8, like.shape[3]))


def grouped_gather(value, groups, place):
    size = len(groups[0])
    parts = [value]
    for shift in range(1, size):
        pairs = [(g[k], g[(k + shift) % size]) for g in groups for k in range(size)]
        parts.append(lax.ppermute(value, "seq", pairs))
    sources = (place - jnp.arange(size)) % size
    return jnp.stack(parts), sources


def seq_groups():
    count = lax.axis_size("seq")
    rows = count // ROW
    row_groups = [[z * ROW + x for x in range(ROW)] for z in range(rows)]
    col_groups = [[z * ROW + x for z in range(rows)] for x in range(ROW)]
    return row_groups, col_groups


def prefix_state(final, log_carry):
    place = lax.axis_index("seq")
    col, row = place % ROW, place // ROW
    row_groups, col_groups = seq_groups()
    size = final.shape[2]
    row_all, row_ids = grouped_gather(
        jnp.concatenate([final, tile_logs(log_carry, final)], axis=2), row_groups, col
    )
    row_logs = jnp.max(row_all[:, :, :, size:], axis=(3, 4))
    in_row = weighted_sum(gap_weights(row_logs, col, False, row_ids), row_all)[:, :, :size]
    row_total = weighted_sum(gap_weights(row_logs, ROW, False, row_ids), row_all)[:, :, :size]
    row_log = jnp.sum(row_logs, axis=0)
    col_all, col_ids = grouped_gather(
        jnp.concatenate([row_total, tile_logs(row_log, final)], axis=2), col_groups, row
    )
    col_logs = jnp.max(col_all[:, :, :, size:], axis=(3, 4))
    before_row = weighted_sum(gap_weights(col_logs, row, False, col_ids), col_all)[:, :, :size]
    into_row = jnp.sum(jnp.where((row_ids < col)[:, None, None], row_logs, 0.0), axis=0)
    incoming = in_row + jnp.exp(into_row)[..., None, None] * before_row
    return incoming, (row_logs, row_ids, col_logs, col_ids)


def suffix_state(leaving, logs):
    row_logs, row_ids, col_logs, col_ids = logs
    place = lax.axis_index("seq")
    col, row = place % ROW, place // ROW
    row_groups, col_groups = seq_groups()
    row_all = grouped_gather(leaving, row_groups, col)[0]
    in_row = weighted_sum(gap_weights(row_logs, col, True, row_ids), row_all)
    row_head = weighted_sum(gap_weights(row_logs, -1, True, row_ids), row_all)
    col_all = grouped_gather(row_head, col_groups, row)[0]
    after_row = weighted_sum(gap_weights(col_logs, row, True, col_ids), col_all)
    out_of_row = jnp.sum(jnp.where((row_ids > col)[:, None, None], row_logs, 0.0), axis=0)
    return in_row + jnp.exp(out_of_row)[..., None, None] * after_row


def head_sum(values):
    count = lax.axis_size("head")
    if count & (count - 1):
        return lax.psum(values, "head")
    shift = 1
    while shift < count:
        pairs = [(i, i ^ shift) for i in range(count)]
        values = values + lax.ppermute(values, "head", pairs)
        shift *= 2
    return values


def weighted_sum(weights, states):
    total = weights[0][..., None, None] * states[0]
    for source in range(1, states.shape[0]):
        total = total + weights[source][..., None, None] * states[source]
    return total


def pair_scores(c_half, b_half):
    return jnp.einsum("kign,kjgn->kgij", c_half, b_half, preferred_element_type=jnp.float32)


def score_grads(grad_scores, b_blocks, c_blocks):
    grad_c = jnp.einsum("kgij,kjgn->kign", grad_scores, b_blocks, precision=PRECISION)
    grad_b = jnp.einsum("kgij,kign->kjgn", grad_scores, c_blocks, precision=PRECISION)
    return (grad_b, grad_c)


def block_chain(x_blocks, a_blocks, b_blocks):
    length = a_blocks.shape[1]
    ids = jnp.arange(length)
    lower = (ids[:, None] >= ids[None, :]).astype(jnp.float32)
    running = jnp.einsum("kjgr,ij->kgri", a_blocks, lower, precision=EXACT)
    span_end = running[..., -1]
    to_end = jnp.exp(span_end[..., None] - running)
    scaled = x_blocks * jnp.moveaxis(to_end, 3, 1)[..., None]
    block_states = jnp.einsum("kjgrp,kjgn->kgrpn", scaled, b_blocks, precision=PRECISION)
    factors = jnp.exp(span_end)
    carried = jnp.zeros(block_states.shape[1:], jnp.float32)
    start_list = []
    for block in range(block_states.shape[0]):
        start_list.append(carried)
        carried = factors[block][..., None, None] * carried + block_states[block]
    return (running, span_end, jnp.stack(start_list), carried)


def local_core(x_blocks, a_blocks, b_blocks, c_blocks, scores):
    running, span_end, starts, _ = block_chain(x_blocks, a_blocks, b_blocks)
    length = running.shape[3]
    row_numbers = lax.broadcasted_iota(jnp.int32, (length, length), 0)
    col_ids = lax.broadcasted_iota(jnp.int32, (length, length), 1)
    causal = row_numbers >= col_ids
    log_gaps = running[..., :, None] - running[..., None, :]
    decays = jnp.exp(jnp.where(causal, log_gaps, -1e30))
    weighted = decays * scores[:, :, None]
    diagonal = jnp.einsum("kgrij,kjgrp->kigrp", weighted, x_blocks, precision=PRECISION)
    from_state = jnp.einsum("kign,kgrpn->kigrp", c_blocks, starts, precision=PRECISION)
    ssd_part = diagonal + from_state * jnp.moveaxis(jnp.exp(running), 3, 1)[..., None]
    earlier = jnp.cumsum(span_end, axis=0) - span_end
    reach = jnp.exp(running + earlier[..., None])
    return (ssd_part, reach)


def edge_grads(adjoint, carry_grad, x_blocks, b_blocks, to_end, later, carry_all):
    tokens = x_blocks.shape[0] * x_blocks.shape[1]
    x_tok = x_blocks.reshape((tokens,) + x_blocks.shape[2:])
    b_tok = b_blocks.reshape((tokens,) + b_blocks.shape[2:])
    weights = jnp.exp(jnp.moveaxis(to_end + later[..., None], 3, 1))
    weights = weights.reshape((tokens,) + weights.shape[2:])
    projected = jnp.einsum("tgn,grpn->tgrp", b_tok, adjoint, precision=PRECISION)
    grad_x = weights[..., None] * projected
    log_grad = weights * jnp.sum(x_tok * projected, axis=3)
    grad_b = jnp.einsum("tgrp,grpn->tgn", weights[..., None] * x_tok, adjoint, precision=PRECISION)
    ids = jnp.arange(tokens)
    strict = (ids[:, None] > ids[None, :]).astype(jnp.float32)
    before = jnp.einsum("tgr,st->sgr", log_grad, strict, precision=EXACT)
    grad_a = before + (carry_grad * carry_all)[None]
    return (
        grad_x.reshape(x_blocks.shape),
        grad_a.reshape(x_blocks.shape[:4]),
        grad_b.reshape(b_blocks.shape),
    )


def add_incoming(ssd_part, reach, c_blocks, incoming):
    projected = jnp.einsum("kign,grpn->kigrp", c_blocks, incoming, precision=PRECISION)
    return ssd_part + projected * jnp.moveaxis(reach, 3, 1)[..., None]


def device_body(inputs, gate_input, log_decay, b_matrix, c_matrix, norm_gain, cotangent):
    tok_rows, width = inputs.shape
    head_count = log_decay.shape[1]
    groups = b_matrix.shape[1]
    state_size = b_matrix.shape[2]
    head_size = width // head_count
    per_group = head_count // groups
    blocks = tok_rows // SPAN
    full_width = width * lax.axis_size("head")
    x_blocks = inputs.astype(jnp.float32).reshape(blocks, SPAN, groups, per_group, head_size)
    a_blocks = log_decay.reshape(blocks, SPAN, groups, per_group)
    b_half = b_matrix.reshape(blocks, SPAN, groups, state_size)
    c_half = c_matrix.reshape(blocks, SPAN, groups, state_size)
    b_blocks = b_half.astype(jnp.float32)
    c_blocks = c_half.astype(jnp.float32)
    scores = pair_scores(c_half, b_half)
    core_out, core_pull = jax.vjp(local_core, x_blocks, a_blocks, b_blocks, c_blocks, scores)
    ssd_part, reach = core_out
    ssd_part = lax.optimization_barrier(ssd_part)
    running, span_end, _, _ = block_chain(x_blocks, a_blocks, b_blocks)
    carry_all = jnp.exp(jnp.sum(span_end, axis=0))
    to_end = span_end[..., None] - running
    later = jnp.cumsum(span_end[::-1], axis=0)[::-1] - span_end
    token_weights = jnp.exp(jnp.moveaxis(to_end + later[..., None], 3, 1)).reshape(
        tok_rows, groups, per_group
    )
    weighted_x = inputs.astype(jnp.float32).reshape(tok_rows, groups, per_group, head_size)
    final = jnp.einsum(
        "tgrp,tgn->grpn",
        weighted_x * token_weights[..., None],
        b_matrix.astype(jnp.float32),
        precision=PRECISION,
    )
    log_carry = jnp.sum(a_blocks, axis=(0, 1))
    incoming, seq_logs = prefix_state(final, log_carry)

    def light_step(part_a, part_b, part_c):
        return add_incoming(part_a, part_b, part_c, incoming)

    light_out, light_pull = jax.vjp(light_step, ssd_part, reach, c_blocks)
    ssd_out = light_out.reshape(tok_rows, width)
    gate_value = gate_input.astype(jnp.float32)
    sigmoid_gate = jax.nn.sigmoid(gate_value)
    gate_silu = gate_value * sigmoid_gate
    scaled_cot = norm_gain[None, :] * cotangent.astype(jnp.float32)
    gated = ssd_out * gate_silu
    squares, products = head_sum(
        jnp.stack([jnp.sum(gated * gated, axis=1), jnp.sum(gated * scaled_cot, axis=1)])
    )
    inverse_rms = lax.rsqrt(squares / full_width + EPSILON)
    normed = (gated * inverse_rms[:, None] * norm_gain[None, :]).astype(jnp.bfloat16)
    grad_gated = (
        inverse_rms[:, None] * scaled_cot
        - gated * (inverse_rms**3 * products / full_width)[:, None]
    )
    grad_gate = (
        grad_gated * ssd_out * sigmoid_gate * (1.0 + gate_value * (1.0 - sigmoid_gate))
    ).astype(jnp.bfloat16)
    grad_ssd = grad_gated * gate_silu
    upstream = grad_ssd.reshape(blocks, SPAN, groups, per_group, head_size)
    reached = upstream * jnp.moveaxis(reach, 3, 1)[..., None]
    leaving = jnp.einsum("kign,kigrp->grpn", c_blocks, reached, precision=PRECISION)
    adjoint = suffix_state(leaving, seq_logs)
    light_grads = light_pull(upstream)
    core_grads = lax.optimization_barrier(core_pull(tuple(light_grads[:2])))
    carry_grad = jnp.sum(adjoint * incoming, axis=(2, 3))
    edge_x, edge_a, edge_b = edge_grads(
        adjoint, carry_grad, x_blocks, b_blocks, to_end, later, carry_all
    )
    grad_x_core, grad_a_core, grad_b_core, grad_c_core, grad_scores = core_grads
    extra_b, extra_c = score_grads(grad_scores, b_blocks, c_blocks)
    grad_x = grad_x_core + edge_x
    grad_a = grad_a_core + edge_a
    grad_b = grad_b_core + extra_b + edge_b
    grad_c = grad_c_core + extra_c + light_grads[2]
    grad_inputs = grad_x.reshape(tok_rows, width).astype(jnp.bfloat16)
    grad_decay = grad_a.reshape(tok_rows, head_count)
    grad_b_matrix = grad_b.reshape(tok_rows, groups, state_size)
    grad_c_matrix = grad_c.reshape(tok_rows, groups, state_size)
    return (normed, grad_inputs, grad_gate, grad_decay, grad_b_matrix, grad_c_matrix)


def solution(mesh):
    placed = (
        P("seq", "head"),
        P("seq", "head"),
        P("seq", "head"),
        P("seq", "head", None),
        P("seq", "head", None),
        P("head"),
        P("seq", "head"),
    )
    return jax.shard_map(
        device_body,
        mesh=mesh,
        in_specs=placed,
        out_specs=(
            P("seq", "head"),
            P("seq", "head"),
            P("seq", "head"),
            P("seq", "head"),
            P("seq", "head", None),
            P("seq", "head", None),
        ),
        check_vma=False,
    )
```

```python
import jax
import jax.numpy as jnp
from jax import lax
from jax.sharding import PartitionSpec as P


SPAN = 128


PRECISION = lax.Precision.HIGH
EXACT = lax.Precision.HIGHEST
EPSILON = 1e-05


ROW = 4


def gap_weights(log_carry, place, later, ids=None):
    if ids is None:
        ids = jnp.arange(log_carry.shape[0])
    if later:
        source_ok = ids > place
        between = (ids[None, :] > place) & (ids[None, :] < ids[:, None])
    else:
        source_ok = ids < place
        between = (ids[None, :] > ids[:, None]) & (ids[None, :] < place)
    log_gap = jnp.sum(jnp.where(between[:, :, None, None], log_carry[None], 0.0), axis=1)
    return jnp.where(source_ok[:, None, None], jnp.exp(log_gap), 0.0)


def tile_logs(log_carry, like):
    return jnp.broadcast_to(log_carry[..., None, None], like.shape[:2] + (8, like.shape[3]))


def grouped_gather(value, groups, place):
    size = len(groups[0])
    parts = [value]
    for shift in range(1, size):
        pairs = [(g[k], g[(k + shift) % size]) for g in groups for k in range(size)]
        parts.append(lax.ppermute(value, "seq", pairs))
    sources = (place - jnp.arange(size)) % size
    return jnp.stack(parts), sources


def seq_groups():
    count = lax.axis_size("seq")
    rows = count // ROW
    row_groups = [[z * ROW + x for x in range(ROW)] for z in range(rows)]
    col_groups = [[z * ROW + x for z in range(rows)] for x in range(ROW)]
    return row_groups, col_groups


def prefix_state(final, log_carry):
    place = lax.axis_index("seq")
    col, row = place % ROW, place // ROW
    row_groups, col_groups = seq_groups()
    size = final.shape[2]
    row_all, row_ids = grouped_gather(
        jnp.concatenate([final, tile_logs(log_carry, final)], axis=2), row_groups, col
    )
    row_logs = jnp.max(row_all[:, :, :, size:], axis=(3, 4))
    in_row = weighted_sum(gap_weights(row_logs, col, False, row_ids), row_all)[:, :, :size]
    row_total = weighted_sum(gap_weights(row_logs, ROW, False, row_ids), row_all)[:, :, :size]
    row_log = jnp.sum(row_logs, axis=0)
    col_all, col_ids = grouped_gather(
        jnp.concatenate([row_total, tile_logs(row_log, final)], axis=2), col_groups, row
    )
    col_logs = jnp.max(col_all[:, :, :, size:], axis=(3, 4))
    before_row = weighted_sum(gap_weights(col_logs, row, False, col_ids), col_all)[:, :, :size]
    into_row = jnp.sum(jnp.where((row_ids < col)[:, None, None], row_logs, 0.0), axis=0)
    incoming = in_row + jnp.exp(into_row)[..., None, None] * before_row
    return incoming, (row_logs, row_ids, col_logs, col_ids)


def suffix_state(leaving, logs):
    row_logs, row_ids, col_logs, col_ids = logs
    place = lax.axis_index("seq")
    col, row = place % ROW, place // ROW
    row_groups, col_groups = seq_groups()
    row_all = grouped_gather(leaving, row_groups, col)[0]
    in_row = weighted_sum(gap_weights(row_logs, col, True, row_ids), row_all)
    row_head = weighted_sum(gap_weights(row_logs, -1, True, row_ids), row_all)
    col_all = grouped_gather(row_head, col_groups, row)[0]
    after_row = weighted_sum(gap_weights(col_logs, row, True, col_ids), col_all)
    out_of_row = jnp.sum(jnp.where((row_ids > col)[:, None, None], row_logs, 0.0), axis=0)
    return in_row + jnp.exp(out_of_row)[..., None, None] * after_row


def head_sum(values):
    count = lax.axis_size("head")
    if count & (count - 1):
        return lax.psum(values, "head")
    shift = 1
    while shift < count:
        pairs = [(i, i ^ shift) for i in range(count)]
        values = values + lax.ppermute(values, "head", pairs)
        shift *= 2
    return values


def weighted_sum(weights, states):
    total = weights[0][..., None, None] * states[0]
    for source in range(1, states.shape[0]):
        total = total + weights[source][..., None, None] * states[source]
    return total


def pair_scores(c_half, b_half):
    return jnp.einsum("kign,kjgn->kgij", c_half, b_half, preferred_element_type=jnp.float32)


def score_grads(grad_scores, b_blocks, c_blocks):
    grad_c = jnp.einsum("kgij,kjgn->kign", grad_scores, b_blocks, precision=PRECISION)
    grad_b = jnp.einsum("kgij,kign->kjgn", grad_scores, c_blocks, precision=PRECISION)
    return (grad_b, grad_c)


def block_chain(x_blocks, a_blocks, b_blocks):
    length = a_blocks.shape[1]
    ids = jnp.arange(length)
    lower = (ids[:, None] >= ids[None, :]).astype(jnp.float32)
    running = jnp.einsum("kjgr,ij->kgri", a_blocks, lower, precision=EXACT)
    span_end = running[..., -1]
    to_end = jnp.exp(span_end[..., None] - running)
    scaled = x_blocks * jnp.moveaxis(to_end, 3, 1)[..., None]
    block_states = jnp.einsum("kjgrp,kjgn->kgrpn", scaled, b_blocks, precision=PRECISION)
    factors = jnp.exp(span_end)
    carried = jnp.zeros(block_states.shape[1:], jnp.float32)
    start_list = []
    for block in range(block_states.shape[0]):
        start_list.append(carried)
        carried = factors[block][..., None, None] * carried + block_states[block]
    return (running, span_end, jnp.stack(start_list), carried)


def local_core(x_blocks, a_blocks, b_blocks, c_blocks, scores):
    running, span_end, starts, _ = block_chain(x_blocks, a_blocks, b_blocks)
    length = running.shape[3]
    row_numbers = lax.broadcasted_iota(jnp.int32, (length, length), 0)
    col_ids = lax.broadcasted_iota(jnp.int32, (length, length), 1)
    causal = row_numbers >= col_ids
    log_gaps = running[..., :, None] - running[..., None, :]
    decays = jnp.exp(jnp.where(causal, log_gaps, -1e30))
    weighted = decays * scores[:, :, None]
    diagonal = jnp.einsum("kgrij,kjgrp->kigrp", weighted, x_blocks, precision=PRECISION)
    from_state = jnp.einsum("kign,kgrpn->kigrp", c_blocks, starts, precision=PRECISION)
    ssd_part = diagonal + from_state * jnp.moveaxis(jnp.exp(running), 3, 1)[..., None]
    earlier = jnp.cumsum(span_end, axis=0) - span_end
    reach = jnp.exp(running + earlier[..., None])
    return (ssd_part, reach)


def edge_grads(adjoint, carry_grad, x_blocks, b_blocks, to_end, later, carry_all):
    tokens = x_blocks.shape[0] * x_blocks.shape[1]
    x_tok = x_blocks.reshape((tokens,) + x_blocks.shape[2:])
    b_tok = b_blocks.reshape((tokens,) + b_blocks.shape[2:])
    weights = jnp.exp(jnp.moveaxis(to_end + later[..., None], 3, 1))
    weights = weights.reshape((tokens,) + weights.shape[2:])
    projected = jnp.einsum("tgn,grpn->tgrp", b_tok, adjoint, precision=PRECISION)
    grad_x = weights[..., None] * projected
    log_grad = weights * jnp.sum(x_tok * projected, axis=3)
    grad_b = jnp.einsum("tgrp,grpn->tgn", weights[..., None] * x_tok, adjoint, precision=PRECISION)
    ids = jnp.arange(tokens)
    strict = (ids[:, None] > ids[None, :]).astype(jnp.float32)
    before = jnp.einsum("tgr,st->sgr", log_grad, strict, precision=EXACT)
    grad_a = before + (carry_grad * carry_all)[None]
    return (
        grad_x.reshape(x_blocks.shape),
        grad_a.reshape(x_blocks.shape[:4]),
        grad_b.reshape(b_blocks.shape),
    )


def add_incoming(ssd_part, reach, c_blocks, incoming):
    projected = jnp.einsum("kign,grpn->kigrp", c_blocks, incoming, precision=PRECISION)
    return ssd_part + projected * jnp.moveaxis(reach, 3, 1)[..., None]


def device_body(inputs, gate_input, log_decay, b_matrix, c_matrix, norm_gain, cotangent):
    tok_rows, width = inputs.shape
    head_count = log_decay.shape[1]
    groups = b_matrix.shape[1]
    state_size = b_matrix.shape[2]
    head_size = width // head_count
    per_group = head_count // groups
    blocks = tok_rows // SPAN
    full_width = width * lax.axis_size("head")
    x_blocks = inputs.astype(jnp.float32).reshape(blocks, SPAN, groups, per_group, head_size)
    a_blocks = log_decay.reshape(blocks, SPAN, groups, per_group)
    b_half = b_matrix.reshape(blocks, SPAN, groups, state_size)
    c_half = c_matrix.reshape(blocks, SPAN, groups, state_size)
    b_blocks = b_half.astype(jnp.float32)
    c_blocks = c_half.astype(jnp.float32)
    scores = pair_scores(c_half, b_half)
    core_out, core_pull = jax.vjp(local_core, x_blocks, a_blocks, b_blocks, c_blocks, scores)
    ssd_part, reach = core_out
    ssd_part = lax.optimization_barrier(ssd_part)
    running, span_end, _, _ = block_chain(x_blocks, a_blocks, b_blocks)
    carry_all = jnp.exp(jnp.sum(span_end, axis=0))
    to_end = span_end[..., None] - running
    later = jnp.cumsum(span_end[::-1], axis=0)[::-1] - span_end
    token_weights = jnp.exp(jnp.moveaxis(to_end + later[..., None], 3, 1)).reshape(
        tok_rows, groups, per_group
    )
    weighted_x = inputs.astype(jnp.float32).reshape(tok_rows, groups, per_group, head_size)
    final = jnp.einsum(
        "tgrp,tgn->grpn",
        weighted_x * token_weights[..., None],
        b_matrix.astype(jnp.float32),
        precision=PRECISION,
    )
    log_carry = jnp.sum(a_blocks, axis=(0, 1))
    incoming, seq_logs = prefix_state(final, log_carry)

    def light_step(part_a, part_b, part_c):
        return add_incoming(part_a, part_b, part_c, incoming)

    light_out, light_pull = jax.vjp(light_step, ssd_part, reach, c_blocks)
    ssd_out = light_out.reshape(tok_rows, width)
    gate_value = gate_input.astype(jnp.float32)
    sigmoid_gate = jax.nn.sigmoid(gate_value)
    gate_silu = gate_value * sigmoid_gate
    scaled_cot = norm_gain[None, :] * cotangent.astype(jnp.float32)
    gated = ssd_out * gate_silu
    squares, products = head_sum(
        jnp.stack([jnp.sum(gated * gated, axis=1), jnp.sum(gated * scaled_cot, axis=1)])
    )
    inverse_rms = lax.rsqrt(squares / full_width + EPSILON)
    normed = (gated * inverse_rms[:, None] * norm_gain[None, :]).astype(jnp.bfloat16)
    grad_gated = (
        inverse_rms[:, None] * scaled_cot
        - gated * (inverse_rms**3 * products / full_width)[:, None]
    )
    grad_gate = (
        grad_gated * ssd_out * sigmoid_gate * (1.0 + gate_value * (1.0 - sigmoid_gate))
    ).astype(jnp.bfloat16)
    grad_ssd = grad_gated * gate_silu
    upstream = grad_ssd.reshape(blocks, SPAN, groups, per_group, head_size)
    reach_tok = jnp.moveaxis(reach, 3, 1).reshape(tok_rows, groups, per_group)
    reached = grad_ssd.reshape(tok_rows, groups, per_group, head_size) * reach_tok[..., None]
    leaving = jnp.einsum(
        "tgrp,tgn->grpn", reached, c_matrix.astype(jnp.float32), precision=PRECISION
    )
    adjoint = suffix_state(leaving, seq_logs)
    light_grads = light_pull(upstream)
    core_grads = lax.optimization_barrier(core_pull(tuple(light_grads[:2])))
    carry_grad = jnp.sum(adjoint * incoming, axis=(2, 3))
    edge_x, edge_a, edge_b = edge_grads(
        adjoint, carry_grad, x_blocks, b_blocks, to_end, later, carry_all
    )
    grad_x_core, grad_a_core, grad_b_core, grad_c_core, grad_scores = core_grads
    extra_b, extra_c = score_grads(grad_scores, b_blocks, c_blocks)
    grad_x = grad_x_core + edge_x
    grad_a = grad_a_core + edge_a
    grad_b = grad_b_core + extra_b + edge_b
    grad_c = grad_c_core + extra_c + light_grads[2]
    grad_inputs = grad_x.reshape(tok_rows, width).astype(jnp.bfloat16)
    grad_decay = grad_a.reshape(tok_rows, head_count)
    grad_b_matrix = grad_b.reshape(tok_rows, groups, state_size)
    grad_c_matrix = grad_c.reshape(tok_rows, groups, state_size)
    return (normed, grad_inputs, grad_gate, grad_decay, grad_b_matrix, grad_c_matrix)


def solution(mesh):
    placed = (
        P("seq", "head"),
        P("seq", "head"),
        P("seq", "head"),
        P("seq", "head", None),
        P("seq", "head", None),
        P("head"),
        P("seq", "head"),
    )
    return jax.shard_map(
        device_body,
        mesh=mesh,
        in_specs=placed,
        out_specs=(
            P("seq", "head"),
            P("seq", "head"),
            P("seq", "head"),
            P("seq", "head"),
            P("seq", "head", None),
            P("seq", "head", None),
        ),
        check_vma=False,
    )
```

```python
import jax
import jax.numpy as jnp
from jax import lax
from jax.sharding import PartitionSpec as P


SPAN = 128


PRECISION = lax.Precision.HIGH
EXACT = lax.Precision.HIGHEST
EPSILON = 1e-05


ROW = 4


def gap_weights(log_carry, place, later, ids=None):
    if ids is None:
        ids = jnp.arange(log_carry.shape[0])
    if later:
        source_ok = ids > place
        between = (ids[None, :] > place) & (ids[None, :] < ids[:, None])
    else:
        source_ok = ids < place
        between = (ids[None, :] > ids[:, None]) & (ids[None, :] < place)
    log_gap = jnp.sum(jnp.where(between[:, :, None, None], log_carry[None], 0.0), axis=1)
    return jnp.where(source_ok[:, None, None], jnp.exp(log_gap), 0.0)


def tile_logs(log_carry, like):
    return jnp.broadcast_to(log_carry[..., None, None], like.shape[:2] + (8, like.shape[3]))


def grouped_gather(value, groups, place, keep=None):
    size = len(groups[0])
    parts = [value]
    for shift in range(1, size):
        ks = range(size)
        if keep == "earlier":
            ks = [k for k in ks if k + shift < size]
        elif keep == "later":
            ks = [k for k in ks if k + shift >= size]
        pairs = [(g[k], g[(k + shift) % size]) for g in groups for k in ks]
        parts.append(lax.ppermute(value, "seq", pairs))
    sources = (place - jnp.arange(size)) % size
    return jnp.stack(parts), sources


def seq_groups():
    count = lax.axis_size("seq")
    rows = count // ROW
    row_groups = [[z * ROW + x for x in range(ROW)] for z in range(rows)]
    col_groups = [[z * ROW + x for z in range(rows)] for x in range(ROW)]
    return row_groups, col_groups


def prefix_state(final, log_carry):
    place = lax.axis_index("seq")
    col, row = place % ROW, place // ROW
    row_groups, col_groups = seq_groups()
    size = final.shape[2]
    row_all, row_ids = grouped_gather(
        jnp.concatenate([final, tile_logs(log_carry, final)], axis=2), row_groups, col
    )
    row_logs = jnp.max(row_all[:, :, :, size:], axis=(3, 4))
    in_row = weighted_sum(gap_weights(row_logs, col, False, row_ids), row_all)[:, :, :size]
    row_total = weighted_sum(gap_weights(row_logs, ROW, False, row_ids), row_all)[:, :, :size]
    row_log = jnp.sum(row_logs, axis=0)
    col_all, col_ids = grouped_gather(
        jnp.concatenate([row_total, tile_logs(row_log, final)], axis=2),
        col_groups,
        row,
    )
    col_logs = jnp.max(col_all[:, :, :, size:], axis=(3, 4))
    before_row = weighted_sum(gap_weights(col_logs, row, False, col_ids), col_all)[:, :, :size]
    into_row = jnp.sum(jnp.where((row_ids < col)[:, None, None], row_logs, 0.0), axis=0)
    incoming = in_row + jnp.exp(into_row)[..., None, None] * before_row
    return incoming, (row_logs, row_ids, col_logs, col_ids)


def suffix_state(leaving, logs):
    row_logs, row_ids, col_logs, col_ids = logs
    place = lax.axis_index("seq")
    col, row = place % ROW, place // ROW
    row_groups, col_groups = seq_groups()
    row_all = grouped_gather(leaving, row_groups, col)[0]
    in_row = weighted_sum(gap_weights(row_logs, col, True, row_ids), row_all)
    row_head = weighted_sum(gap_weights(row_logs, -1, True, row_ids), row_all)
    col_all = grouped_gather(row_head, col_groups, row, "later")[0]
    after_row = weighted_sum(gap_weights(col_logs, row, True, col_ids), col_all)
    out_of_row = jnp.sum(jnp.where((row_ids > col)[:, None, None], row_logs, 0.0), axis=0)
    return in_row + jnp.exp(out_of_row)[..., None, None] * after_row


def head_sum(values):
    count = lax.axis_size("head")
    if count & (count - 1):
        return lax.psum(values, "head")
    shift = 1
    while shift < count:
        pairs = [(i, i ^ shift) for i in range(count)]
        values = values + lax.ppermute(values, "head", pairs)
        shift *= 2
    return values


def weighted_sum(weights, states):
    total = weights[0][..., None, None] * states[0]
    for source in range(1, states.shape[0]):
        total = total + weights[source][..., None, None] * states[source]
    return total


def pair_scores(c_half, b_half):
    return jnp.einsum("kign,kjgn->kgij", c_half, b_half, preferred_element_type=jnp.float32)


def score_grads(grad_scores, b_blocks, c_blocks):
    grad_c = jnp.einsum("kgij,kjgn->kign", grad_scores, b_blocks, precision=PRECISION)
    grad_b = jnp.einsum("kgij,kign->kjgn", grad_scores, c_blocks, precision=PRECISION)
    return (grad_b, grad_c)


def block_chain(x_blocks, a_blocks, b_blocks):
    length = a_blocks.shape[1]
    ids = jnp.arange(length)
    lower = (ids[:, None] >= ids[None, :]).astype(jnp.float32)
    running = jnp.einsum("kjgr,ij->kgri", a_blocks, lower, precision=EXACT)
    span_end = running[..., -1]
    to_end = jnp.exp(span_end[..., None] - running)
    scaled = x_blocks * jnp.moveaxis(to_end, 3, 1)[..., None]
    block_states = jnp.einsum("kjgrp,kjgn->kgrpn", scaled, b_blocks, precision=PRECISION)
    factors = jnp.exp(span_end)
    carried = jnp.zeros(block_states.shape[1:], jnp.float32)
    start_list = []
    for block in range(block_states.shape[0]):
        start_list.append(carried)
        carried = factors[block][..., None, None] * carried + block_states[block]
    return (running, span_end, jnp.stack(start_list), carried)


def local_core(x_blocks, a_blocks, b_blocks, c_blocks, scores):
    running, span_end, starts, _ = block_chain(x_blocks, a_blocks, b_blocks)
    length = running.shape[3]
    row_numbers = lax.broadcasted_iota(jnp.int32, (length, length), 0)
    col_ids = lax.broadcasted_iota(jnp.int32, (length, length), 1)
    causal = row_numbers >= col_ids
    log_gaps = running[..., :, None] - running[..., None, :]
    decays = jnp.exp(jnp.where(causal, log_gaps, -1e30))
    weighted = decays * scores[:, :, None]
    diagonal = jnp.einsum("kgrij,kjgrp->kigrp", weighted, x_blocks, precision=PRECISION)
    from_state = jnp.einsum("kign,kgrpn->kigrp", c_blocks, starts, precision=PRECISION)
    ssd_part = diagonal + from_state * jnp.moveaxis(jnp.exp(running), 3, 1)[..., None]
    earlier = jnp.cumsum(span_end, axis=0) - span_end
    reach = jnp.exp(running + earlier[..., None])
    return (ssd_part, reach)


def edge_grads(adjoint, carry_grad, x_blocks, b_blocks, to_end, later, carry_all):
    tokens = x_blocks.shape[0] * x_blocks.shape[1]
    x_tok = x_blocks.reshape((tokens,) + x_blocks.shape[2:])
    b_tok = b_blocks.reshape((tokens,) + b_blocks.shape[2:])
    weights = jnp.exp(jnp.moveaxis(to_end + later[..., None], 3, 1))
    weights = weights.reshape((tokens,) + weights.shape[2:])
    projected = jnp.einsum("tgn,grpn->tgrp", b_tok, adjoint, precision=PRECISION)
    grad_x = weights[..., None] * projected
    log_grad = weights * jnp.sum(x_tok * projected, axis=3)
    grad_b = jnp.einsum("tgrp,grpn->tgn", weights[..., None] * x_tok, adjoint, precision=PRECISION)
    ids = jnp.arange(tokens)
    strict = (ids[:, None] > ids[None, :]).astype(jnp.float32)
    before = jnp.einsum("tgr,st->sgr", log_grad, strict, precision=EXACT)
    grad_a = before + (carry_grad * carry_all)[None]
    return (
        grad_x.reshape(x_blocks.shape),
        grad_a.reshape(x_blocks.shape[:4]),
        grad_b.reshape(b_blocks.shape),
    )


def add_incoming(ssd_part, reach, c_blocks, incoming):
    projected = jnp.einsum("kign,grpn->kigrp", c_blocks, incoming, precision=PRECISION)
    return ssd_part + projected * jnp.moveaxis(reach, 3, 1)[..., None]


def device_body(inputs, gate_input, log_decay, b_matrix, c_matrix, norm_gain, cotangent):
    tok_rows, width = inputs.shape
    head_count = log_decay.shape[1]
    groups = b_matrix.shape[1]
    state_size = b_matrix.shape[2]
    head_size = width // head_count
    per_group = head_count // groups
    blocks = tok_rows // SPAN
    full_width = width * lax.axis_size("head")
    x_blocks = inputs.astype(jnp.float32).reshape(blocks, SPAN, groups, per_group, head_size)
    a_blocks = log_decay.reshape(blocks, SPAN, groups, per_group)
    b_half = b_matrix.reshape(blocks, SPAN, groups, state_size)
    c_half = c_matrix.reshape(blocks, SPAN, groups, state_size)
    b_blocks = b_half.astype(jnp.float32)
    c_blocks = c_half.astype(jnp.float32)
    scores = pair_scores(c_half, b_half)
    core_out, core_pull = jax.vjp(local_core, x_blocks, a_blocks, b_blocks, c_blocks, scores)
    ssd_part, reach = core_out
    ssd_part = lax.optimization_barrier(ssd_part)
    running, span_end, _, _ = block_chain(x_blocks, a_blocks, b_blocks)
    carry_all = jnp.exp(jnp.sum(span_end, axis=0))
    to_end = span_end[..., None] - running
    later = jnp.cumsum(span_end[::-1], axis=0)[::-1] - span_end
    token_weights = jnp.exp(jnp.moveaxis(to_end + later[..., None], 3, 1)).reshape(
        tok_rows, groups, per_group
    )
    weighted_x = inputs.astype(jnp.float32).reshape(tok_rows, groups, per_group, head_size)
    final = jnp.einsum(
        "tgrp,tgn->grpn",
        weighted_x * token_weights[..., None],
        b_matrix.astype(jnp.float32),
        precision=PRECISION,
    )
    log_carry = jnp.sum(a_blocks, axis=(0, 1))
    incoming, seq_logs = prefix_state(final, log_carry)

    def light_step(part_a, part_b, part_c):
        return add_incoming(part_a, part_b, part_c, incoming)

    light_out, light_pull = jax.vjp(light_step, ssd_part, reach, c_blocks)
    ssd_out = light_out.reshape(tok_rows, width)
    gate_value = gate_input.astype(jnp.float32)
    sigmoid_gate = jax.nn.sigmoid(gate_value)
    gate_silu = gate_value * sigmoid_gate
    scaled_cot = norm_gain[None, :] * cotangent.astype(jnp.float32)
    gated = ssd_out * gate_silu
    squares, products = head_sum(
        jnp.stack([jnp.sum(gated * gated, axis=1), jnp.sum(gated * scaled_cot, axis=1)])
    )
    inverse_rms = lax.rsqrt(squares / full_width + EPSILON)
    normed = (gated * inverse_rms[:, None] * norm_gain[None, :]).astype(jnp.bfloat16)
    grad_gated = (
        inverse_rms[:, None] * scaled_cot
        - gated * (inverse_rms**3 * products / full_width)[:, None]
    )
    grad_gate = (
        grad_gated * ssd_out * sigmoid_gate * (1.0 + gate_value * (1.0 - sigmoid_gate))
    ).astype(jnp.bfloat16)
    grad_ssd = grad_gated * gate_silu
    upstream = grad_ssd.reshape(blocks, SPAN, groups, per_group, head_size)
    reached = upstream * jnp.moveaxis(reach, 3, 1)[..., None]
    leaving = jnp.einsum("kign,kigrp->grpn", c_blocks, reached, precision=PRECISION)
    adjoint = suffix_state(leaving, seq_logs)
    light_grads = light_pull(upstream)
    core_grads = lax.optimization_barrier(core_pull(tuple(light_grads[:2])))
    carry_grad = jnp.sum(adjoint * incoming, axis=(2, 3))
    edge_x, edge_a, edge_b = edge_grads(
        adjoint, carry_grad, x_blocks, b_blocks, to_end, later, carry_all
    )
    grad_x_core, grad_a_core, grad_b_core, grad_c_core, grad_scores = core_grads
    extra_b, extra_c = score_grads(grad_scores, b_blocks, c_blocks)
    grad_x = grad_x_core + edge_x
    grad_a = grad_a_core + edge_a
    grad_b = grad_b_core + extra_b + edge_b
    grad_c = grad_c_core + extra_c + light_grads[2]
    grad_inputs = grad_x.reshape(tok_rows, width).astype(jnp.bfloat16)
    grad_decay = grad_a.reshape(tok_rows, head_count)
    grad_b_matrix = grad_b.reshape(tok_rows, groups, state_size)
    grad_c_matrix = grad_c.reshape(tok_rows, groups, state_size)
    return (normed, grad_inputs, grad_gate, grad_decay, grad_b_matrix, grad_c_matrix)


def solution(mesh):
    placed = (
        P("seq", "head"),
        P("seq", "head"),
        P("seq", "head"),
        P("seq", "head", None),
        P("seq", "head", None),
        P("head"),
        P("seq", "head"),
    )
    return jax.shard_map(
        device_body,
        mesh=mesh,
        in_specs=placed,
        out_specs=(
            P("seq", "head"),
            P("seq", "head"),
            P("seq", "head"),
            P("seq", "head"),
            P("seq", "head", None),
            P("seq", "head", None),
        ),
        check_vma=False,
    )
```
